128 devices in a mesh: chan: 8 (over y_hi, x), tm: 16 (over z, y_lo, core).
Axes of the slice: x: 4, y: 4 (y_hi: 2, y_lo: 2; y = y_hi * 2 + y_lo), z: 4, core: 2. Of those that a mesh axis runs over, the one named last changes fastest.
Arguments:
- traces: bfloat16 [128, 1024, 2048], P('tm', 'chan'), may hold values from -6 to 6
- live: int32 [1024], P('chan'), may hold values 0 or 1
Outputs:
- correlations: bfloat16 [1024, 128, 2048], P(('chan', 'tm'))
The draws below stay inside these ranges and needn't reach their ends.
Inputs may be any that keep to these rules, and one draw needn't show every extreme that they name: `live`: 1 marks a usable channel, 0 a dead one.
All inputs are finite; a program needn't handle non-finite values. No bound on the sum of `live` on one device may be relied on, other than what follows from the above.
Results may differ from the reference program's by a relative error of at most 0.0076.
Values may be sent and summed in bfloat16 or wider, within the bound.
No kernel may reach another device: no remote copies, remote signals or barrier semaphores. Data moves between devices by JAX's collectives and lax.ppermute only.
A program may use at most 128 MiB of HBM per device.

```python
import math
import jax
import jax.numpy as jnp
from jax import lax

BLOCK = 128
SAMPLES = 2048
SMOOTH = 4
FREQS = 1024
SEGMENTS = 128
CHANNELS = 1024
N_CHAN = 8


def set_ends(values, own_key, low, largest):
    longest = values.shape.index(max(values.shape))
    spots = []
    for shift in (0, 1):
        where = [jax.random.randint(jax.random.fold_in(own_key, axis), (), 0, length) for axis, length in enumerate(values.shape)]
        where[longest] = (where[longest] + shift) % values.shape[longest]
        spots.append(tuple(where))
    return values.at[spots[0]].set(low).at[spots[1]].set(largest)


def levels(rng, shape, shards, least, high):
    def one(position, shards_of):
        steps = jax.random.uniform(jax.random.fold_in(jax.random.fold_in(rng, 6), position), (shards_of,), jnp.float32, least / len(shards), high / len(shards))
        return jnp.repeat(jnp.exp(steps), shape[position] // shards_of).reshape((-1,) + (1,) * (len(shape) - position - 1))

    loudness = one(*shards[0])
    for cut in shards[1:]:
        loudness = loudness * one(*cut)
    return loudness


def scatter_about(key, dims, scale, limit, cuts=(), kind=jnp.bfloat16):
    loudness = levels(key, dims, cuts, -0.22, 0.18) if cuts else 1.0
    array = jax.random.normal(key, dims, jnp.float32) * scale * loudness
    return jnp.minimum(jnp.maximum(array, -limit), limit).astype(kind)


def setup_inputs(seed: int = 0) -> dict:
    splits = jax.random.split(jax.random.key(seed), 3)
    traces = scatter_about(splits[0], (SEGMENTS, CHANNELS, SAMPLES), 1.0, 6.0, ((0, 16), (1, 8)))
    live = set_ends((jax.random.randint(splits[1], (CHANNELS,), 0, 8) < 7).astype(jnp.int32), jax.random.fold_in(splits[1], 1), 0, 1)
    return {"traces": traces, "live": live}


def column_bins(count, group_width):
    index = jnp.arange(count, dtype=jnp.int32)
    group = index // (2 * group_width)
    within = index % group_width
    is_imag = index // group_width % 2
    return (group * group_width + within, is_imag)

def forward_table(samples, bins, group_width):
    freq, is_imag = column_bins(2 * bins, group_width)
    moments = jnp.arange(samples, dtype=jnp.int32)[:, None]
    phase = (moments * freq[None, :] % samples).astype(jnp.float32) * (2.0 * math.pi / samples)
    return jnp.where(is_imag[None, :] == 1, -jnp.sin(phase), jnp.cos(phase)).astype(jnp.bfloat16)

def inverse_table(samples, bins, group_width, segments):
    freq, is_imag = column_bins(2 * bins, group_width)
    lag = jnp.arange(samples, dtype=jnp.int32) - samples // 2
    phase = jnp.mod(freq[:, None] * lag[None, :], samples).astype(jnp.float32) * (2.0 * math.pi / samples)
    weight = jnp.where(freq == 0, 1.0, 2.0).astype(jnp.float32) / math.sqrt(samples * segments)
    wave = jnp.where(is_imag[:, None] == 1, -jnp.sin(phase), jnp.cos(phase))
    return (weight[:, None] * wave).astype(jnp.bfloat16)

def whiten(spectra, groups):
    lead = spectra.shape[:-1]
    bins = spectra.shape[-1] // 2
    width = bins // groups
    split = spectra.reshape(lead + (groups, 2, width))
    real_part = split[..., 0, :].reshape(lead + (bins,))
    imag_part = split[..., 1, :].reshape(lead + (bins,))
    amplitude = jnp.sqrt(real_part * real_part + imag_part * imag_part)
    padded = jnp.pad(amplitude, [(0, 0)] * len(lead) + [(SMOOTH, SMOOTH)])
    smooth = sum((padded[..., i:i + bins] for i in range(2 * SMOOTH + 1))) / (2 * SMOOTH + 1)
    water = 0.8 * lax.optimization_barrier(jnp.mean(amplitude, axis=-1, keepdims=True)) + 1e-06
    level = jnp.maximum(smooth, water).reshape(lead + (groups, 1, width))
    return (split / level).reshape(lead + (2 * bins,)).astype(jnp.bfloat16)

def band(matrix):
    rows, width, extra = matrix.shape
    flat = matrix.reshape(rows * width, extra)
    flat = jnp.pad(flat, ((0, rows), (0, 0)))
    return flat.reshape(rows, width + 1, extra)[:, 1:rows + 1, :]

def cross(own_white, extended, own_flags, ext_flags, half):
    own_real = own_white[..., :half].astype(jnp.float32)
    own_imag = own_white[..., half:].astype(jnp.float32)
    ext_real = extended[..., :half].astype(jnp.float32)
    ext_imag = extended[..., half:].astype(jnp.float32)
    real_sum = jnp.einsum('sah,sbh->abh', own_real, ext_real) + jnp.einsum('sah,sbh->abh', own_imag, ext_imag)
    imag_sum = jnp.einsum('sah,sbh->abh', own_imag, ext_real) - jnp.einsum('sah,sbh->abh', own_real, ext_imag)
    pair_flags = band((own_flags[:, None] * ext_flags[None, :])[:, :, None])
    both = jnp.concatenate([band(real_sum), band(imag_sum)], axis=-1)
    return (both * pair_flags).astype(jnp.bfloat16)

def reference(traces, live):
    table = forward_table(SAMPLES, FREQS, FREQS)
    inverse = inverse_table(SAMPLES, FREQS, FREQS, SEGMENTS)
    blocks = traces.reshape(SEGMENTS, N_CHAN, BLOCK, SAMPLES).transpose(1, 0, 2, 3)

    def spectra_of(block_traces):
        spectra = jnp.dot(block_traces.reshape(SEGMENTS * BLOCK, SAMPLES), table, preferred_element_type=jnp.float32)
        return whiten(spectra.reshape(SEGMENTS, BLOCK, 2 * FREQS), 1)
    white = lax.map(spectra_of, blocks)
    following = jnp.concatenate([white[1:], jnp.zeros_like(white[:1])], axis=0)
    flags = live.reshape(N_CHAN, BLOCK).astype(jnp.float32)
    flags_next = jnp.concatenate([flags[1:], jnp.zeros_like(flags[:1])], axis=0)

    def correlate(items):
        own_white, next_white, own_flags, next_flags = items
        extended = jnp.concatenate([own_white, next_white], axis=1)
        ext_flags = jnp.concatenate([own_flags, next_flags], axis=0)
        stack = cross(own_white, extended, own_flags, ext_flags, FREQS)
        lagged = jnp.dot(stack.reshape(BLOCK * BLOCK, 2 * FREQS), inverse, preferred_element_type=jnp.float32)
        return lagged.astype(jnp.bfloat16).reshape(BLOCK, BLOCK, SAMPLES)
    result = lax.map(correlate, (white, following, flags, flags_next))
    return result.reshape(CHANNELS, BLOCK, SAMPLES)
```

```python
import math

import jax
import jax.numpy as jnp
import numpy as np
from jax import lax
from jax.sharding import PartitionSpec as P

SMOOTH = 4


def from_behind(block, axis, distance):
    devices = range(lax.axis_size(axis))
    route = [(i - distance, i) for i in devices if i - distance in devices]
    return lax.ppermute(block, axis, route)


def column_bins(count, group_width):
    index = np.arange(count, dtype=np.int64)
    group = index // (2 * group_width)
    within = index % group_width
    is_imag = index // group_width % 2
    return (group * group_width + within, is_imag)


def forward_table(samples, bins, group_width):
    freq, is_imag = column_bins(2 * bins, group_width)
    moments = np.arange(samples, dtype=np.int64)[:, None]
    phase = (moments * freq[None, :] % samples).astype(np.float32) * np.float32(2.0 * math.pi / samples)
    phase = phase.astype(np.float64)
    table = np.where(is_imag[None, :] == 1, -np.sin(phase), np.cos(phase)).astype(np.float32)
    return jnp.asarray(table.astype(jnp.bfloat16))


def inverse_table(samples, bins, group_width, segments):
    freq, is_imag = column_bins(2 * bins, group_width)
    lag = np.arange(samples, dtype=np.int64) - samples // 2
    phase = np.mod(freq[:, None] * lag[None, :], samples).astype(np.float32) * np.float32(
        2.0 * math.pi / samples
    )
    phase = phase.astype(np.float64)
    weight = np.where(freq == 0, 1.0, 2.0).astype(np.float32) / np.float32(math.sqrt(samples * segments))
    wave = np.where(is_imag[:, None] == 1, -np.sin(phase), np.cos(phase)).astype(np.float32)
    return jnp.asarray((weight[:, None] * wave).astype(np.float32).astype(jnp.bfloat16))


def whiten(spectra, groups):
    lead = spectra.shape[:-1]
    bins = spectra.shape[-1] // 2
    width = bins // groups
    split = spectra.reshape(lead + (groups, 2, width))
    real_part = split[..., 0, :].reshape(lead + (bins,))
    imag_part = split[..., 1, :].reshape(lead + (bins,))
    amplitude = jnp.sqrt(real_part * real_part + imag_part * imag_part)
    padded = jnp.pad(amplitude, [(0, 0)] * len(lead) + [(SMOOTH, SMOOTH)])
    smooth = sum((padded[..., i : i + bins] for i in range(2 * SMOOTH + 1))) / (2 * SMOOTH + 1)
    water = 0.8 * jnp.mean(amplitude, axis=-1, keepdims=True) + 1e-06
    level = jnp.maximum(smooth, water).reshape(lead + (groups, 1, width))
    return (split / level).reshape(lead + (2 * bins,)).astype(jnp.bfloat16)


def band(matrix):
    rows, width, extra = matrix.shape
    flat = matrix.reshape(rows * width, extra)
    flat = jnp.pad(flat, ((0, rows), (0, 0)))
    return flat.reshape(rows, width + 1, extra)[:, 1 : rows + 1, :]


def product(left, right):
    return jnp.einsum("sah,sbh->abh", left, right, preferred_element_type=jnp.float32)


def cross(own_white, extended, own_flags, ext_flags, half):
    own_real = own_white[..., :half]
    own_imag = own_white[..., half:]
    ext_real = extended[..., :half]
    ext_imag = extended[..., half:]
    real_sum = product(own_real, ext_real) + product(own_imag, ext_imag)
    imag_sum = product(own_imag, ext_real) - product(own_real, ext_imag)
    pair_flags = band((own_flags[:, None] * ext_flags[None, :])[:, :, None])
    both = jnp.concatenate([band(real_sum), band(imag_sum)], axis=-1)
    return (both * pair_flags).astype(jnp.bfloat16)


def transform_rows(traces_part, table, groups):
    seg_dev, rows, samples = traces_part.shape
    spectra = jnp.dot(
        traces_part.reshape(seg_dev * rows, samples), table, preferred_element_type=jnp.float32
    )
    return whiten(spectra.reshape(seg_dev, rows, table.shape[1]), groups)


def body(traces, live):
    seg_dev, block, samples = traces.shape
    bins = samples // 2
    groups = lax.axis_size("tm")
    group_width = bins // groups
    segments = seg_dev * groups
    table = forward_table(samples, bins, group_width)
    inverse = inverse_table(samples, bins, group_width, segments)
    flags = live.astype(jnp.bfloat16)
    white = transform_rows(traces, table, groups)
    own_white = lax.all_to_all(white, "tm", split_axis=2, concat_axis=0, tiled=True)
    next_white, next_flags = from_behind((own_white, flags), "chan", -1)
    extended = jnp.concatenate([own_white, next_white], axis=1)
    ext_flags = jnp.concatenate([flags, next_flags], axis=0).astype(jnp.float32)
    stack = cross(own_white, extended, flags.astype(jnp.float32), ext_flags, group_width)
    lagged = jnp.einsum(
        "rif,fl->ril",
        lax.all_to_all(stack, "tm", split_axis=0, concat_axis=2, tiled=True),
        inverse,
        preferred_element_type=jnp.float32,
    )
    return lagged.astype(jnp.bfloat16)


def solution(mesh):
    in_specs = (P("tm", "chan", None), P("chan"))
    out_specs = P(("chan", "tm"), None, None)
    return jax.shard_map(body, mesh=mesh, in_specs=in_specs, out_specs=out_specs, check_vma=False)
```

```python
import math

import jax
import jax.numpy as jnp
import numpy as np
from jax import lax
from jax.experimental import pallas as pl
from jax.experimental.pallas import tpu as pltpu
from jax.sharding import PartitionSpec as P

SMOOTH = 4


def from_behind(block, axis, distance):
    devices = range(lax.axis_size(axis))
    route = [(i - distance, i) for i in devices if i - distance in devices]
    return lax.ppermute(block, axis, route)


def column_bins(count, group_width):
    index = np.arange(count, dtype=np.int64)
    group = index // (2 * group_width)
    within = index % group_width
    is_imag = index // group_width % 2
    return (group * group_width + within, is_imag)


def forward_table(samples, bins, group_width):
    freq, is_imag = column_bins(2 * bins, group_width)
    moments = np.arange(samples, dtype=np.int64)[:, None]
    phase = (moments * freq[None, :] % samples).astype(np.float32) * np.float32(2.0 * math.pi / samples)
    phase = phase.astype(np.float64)
    table = np.where(is_imag[None, :] == 1, -np.sin(phase), np.cos(phase)).astype(np.float32)
    return jnp.asarray(table.astype(jnp.bfloat16))


def inverse_table(samples, bins, group_width, segments):
    freq, is_imag = column_bins(2 * bins, group_width)
    lag = np.arange(samples, dtype=np.int64) - samples // 2
    phase = np.mod(freq[:, None] * lag[None, :], samples).astype(np.float32) * np.float32(
        2.0 * math.pi / samples
    )
    phase = phase.astype(np.float64)
    weight = np.where(freq == 0, 1.0, 2.0).astype(np.float32) / np.float32(math.sqrt(samples * segments))
    wave = np.where(is_imag[:, None] == 1, -np.sin(phase), np.cos(phase)).astype(np.float32)
    return jnp.asarray((weight[:, None] * wave).astype(np.float32).astype(jnp.bfloat16))


def whiten_cols(spectra, groups):
    bins = spectra.shape[0] // 2
    width = bins // groups
    rest = spectra.shape[1:]
    split = spectra.reshape((groups, 2, width) + rest)
    real_part = split[:, 0].reshape((bins,) + rest)
    imag_part = split[:, 1].reshape((bins,) + rest)
    amplitude = jnp.sqrt(real_part * real_part + imag_part * imag_part)
    padded = jnp.pad(amplitude, [(SMOOTH, SMOOTH)] + [(0, 0)] * len(rest))
    smooth = sum((padded[i : i + bins] for i in range(2 * SMOOTH + 1))) / (2 * SMOOTH + 1)
    water = 0.8 * jnp.mean(amplitude, axis=0, keepdims=True) + 1e-06
    level = jnp.maximum(smooth, water).reshape((groups, 1, width) + rest)
    return (split / level).reshape(spectra.shape)


def cross_kernel(own_ref, rev_ref, next_rev_ref, out_ref):
    block = own_ref.shape[2]
    wide = 2 * block
    row = lax.broadcasted_iota(jnp.int32, (block, block), 0)
    col = lax.broadcasted_iota(jnp.int32, (block, block), 1)
    flip = (row + col == block - 1).astype(jnp.bfloat16)
    for f in range(own_ref.shape[1]):
        own_real = own_ref[0, f]
        own_imag = own_ref[1, f]
        lhs = jnp.concatenate(
            [
                jnp.concatenate([own_real, own_imag], axis=1),
                jnp.concatenate([own_imag, -own_real], axis=1),
            ],
            axis=0,
        )
        rhs = jnp.concatenate(
            [
                jnp.concatenate([next_rev_ref[0, f], next_rev_ref[1, f]], axis=1),
                jnp.concatenate([rev_ref[0, f], rev_ref[1, f]], axis=1),
            ],
            axis=0,
        )
        both = lax.dot_general(
            lhs, rhs, (((1,), (1,)), ((), ())), preferred_element_type=jnp.float32
        )
        for part in range(2):
            rows = both[part * block : (part + 1) * block]
            sheared = pltpu.roll(rows, 1, 1, stride=1, stride_axis=0)[:, block:]
            ordered = jnp.dot(
                sheared.astype(jnp.bfloat16), flip, preferred_element_type=jnp.float32
            )
            out_ref[part, f] = ordered.astype(out_ref.dtype)


def cross(own_t, rev_t, next_rev_t, bins_per_step=8, interpret=False):
    two, width, block, segs = own_t.shape
    spec = pl.BlockSpec((two, bins_per_step, block, segs), lambda i: (0, i, 0, 0))
    return pl.pallas_call(
        cross_kernel,
        grid=(width // bins_per_step,),
        in_specs=[spec, spec, spec],
        out_specs=pl.BlockSpec((two, bins_per_step, block, block), lambda i: (0, i, 0, 0)),
        out_shape=jax.ShapeDtypeStruct((two, width, block, block), jnp.bfloat16),
        interpret=interpret,
    )(own_t, rev_t, next_rev_t)


def body(traces, live):
    seg_dev, block, samples = traces.shape
    bins = samples // 2
    groups = lax.axis_size("tm")
    group_width = bins // groups
    segments = seg_dev * groups
    table = forward_table(samples, bins, group_width)
    inverse = inverse_table(samples, bins, group_width, segments)
    spectra = jnp.einsum("jat,tc->cja", traces, table, preferred_element_type=jnp.float32)
    flags = live.astype(jnp.float32)
    white = (whiten_cols(spectra, groups) * flags).astype(jnp.bfloat16)
    own = lax.all_to_all(white, "tm", split_axis=0, concat_axis=1, tiled=True)
    own_t = jnp.swapaxes(own, 1, 2).reshape(2, group_width, block, segments)
    rev_t = own_t[:, :, ::-1, :]
    next_rev_t = from_behind(rev_t, "chan", -1)
    stack = cross(own_t, rev_t, next_rev_t).reshape(2 * group_width, block, block)
    gathered = lax.all_to_all(stack, "tm", split_axis=1, concat_axis=0, tiled=True)
    lagged = jnp.einsum("hak,hl->akl", gathered, inverse, preferred_element_type=jnp.float32)
    return lagged.astype(jnp.bfloat16)


def solution(mesh):
    in_specs = (P("tm", "chan", None), P("chan"))
    out_specs = P(("chan", "tm"), None, None)
    return jax.shard_map(body, mesh=mesh, in_specs=in_specs, out_specs=out_specs, check_vma=False)
```

```python
import math

import jax
import jax.numpy as jnp
import numpy as np
from jax import lax
from jax.experimental import pallas as pl
from jax.experimental.pallas import tpu as pltpu
from jax.sharding import PartitionSpec as P

SMOOTH = 4


def from_behind(block, axis, distance):
    devices = range(lax.axis_size(axis))
    route = [(i - distance, i) for i in devices if i - distance in devices]
    return lax.ppermute(block, axis, route)


def column_bins(count, group_width):
    index = np.arange(count, dtype=np.int64)
    group = index // (2 * group_width)
    within = index % group_width
    is_imag = index // group_width % 2
    return (group * group_width + within, is_imag)


def forward_table(samples, bins, group_width):
    freq, is_imag = column_bins(2 * bins, group_width)
    moments = np.arange(samples, dtype=np.int64)[:, None]
    phase = (moments * freq[None, :] % samples).astype(np.float32) * np.float32(2.0 * math.pi / samples)
    phase = phase.astype(np.float64)
    table = np.where(is_imag[None, :] == 1, -np.sin(phase), np.cos(phase)).astype(np.float32)
    return jnp.asarray(table.astype(jnp.bfloat16))


def inverse_table(samples, bins, group_width, segments):
    freq, is_imag = column_bins(2 * bins, group_width)
    lag = np.arange(samples, dtype=np.int64) - samples // 2
    phase = np.mod(freq[:, None] * lag[None, :], samples).astype(np.float32) * np.float32(
        2.0 * math.pi / samples
    )
    phase = phase.astype(np.float64)
    weight = np.where(freq == 0, 1.0, 2.0).astype(np.float32) / np.float32(math.sqrt(samples * segments))
    wave = np.where(is_imag[:, None] == 1, -np.sin(phase), np.cos(phase)).astype(np.float32)
    return jnp.asarray((weight[:, None] * wave).astype(np.float32).astype(jnp.bfloat16))


def whiten_cols(spectra, groups):
    bins = spectra.shape[0] // 2
    width = bins // groups
    rest = spectra.shape[1:]
    split = spectra.reshape((groups, 2, width) + rest)
    real_part = split[:, 0].reshape((bins,) + rest)
    imag_part = split[:, 1].reshape((bins,) + rest)
    amplitude = jnp.sqrt(real_part * real_part + imag_part * imag_part)
    padded = jnp.pad(amplitude, [(SMOOTH, SMOOTH)] + [(0, 0)] * len(rest))
    smooth = sum((padded[i : i + bins] for i in range(2 * SMOOTH + 1))) / (2 * SMOOTH + 1)
    water = 0.8 * jnp.mean(amplitude, axis=0, keepdims=True) + 1e-06
    level = jnp.maximum(smooth, water).reshape((groups, 1, width) + rest)
    return (split / level).reshape(spectra.shape)


def cross_kernel(own_ref, next_ref, out_ref):
    block = own_ref.shape[2]
    row = lax.broadcasted_iota(jnp.int32, (block, block), 0)
    col = lax.broadcasted_iota(jnp.int32, (block, block), 1)
    flip = (row + col == block - 1).astype(jnp.bfloat16)

    def reverse_rows(x):
        return jnp.dot(flip, x, preferred_element_type=jnp.float32).astype(jnp.bfloat16)

    for f in range(own_ref.shape[1]):
        own_real = own_ref[0, f]
        own_imag = own_ref[1, f]
        own_both = jnp.concatenate([own_real, own_imag], axis=1)
        lhs = jnp.concatenate(
            [own_both, jnp.concatenate([own_imag, -own_real], axis=1)], axis=0
        )
        next_both = jnp.concatenate([next_ref[0, f], next_ref[1, f]], axis=1)
        rhs = jnp.concatenate([reverse_rows(next_both), reverse_rows(own_both)], axis=0)
        both = lax.dot_general(
            lhs, rhs, (((1,), (1,)), ((), ())), preferred_element_type=jnp.float32
        )
        for part in range(2):
            rows = both[part * block : (part + 1) * block]
            sheared = pltpu.roll(rows, 1, 1, stride=1, stride_axis=0)[:, block:]
            ordered = jnp.dot(
                sheared.astype(jnp.bfloat16), flip, preferred_element_type=jnp.float32
            )
            out_ref[part, f] = ordered.astype(out_ref.dtype)


def cross(own_t, next_t, interpret=False):
    two, width, block, segs = own_t.shape
    step = min(width, 8)
    spec = pl.BlockSpec((two, step, block, segs), lambda i: (0, i, 0, 0))
    return pl.pallas_call(
        cross_kernel,
        grid=(width // step,),
        in_specs=[spec, spec],
        out_specs=pl.BlockSpec((two, step, block, block), lambda i: (0, i, 0, 0)),
        out_shape=jax.ShapeDtypeStruct((two, width, block, block), jnp.bfloat16),
        interpret=interpret,
    )(own_t, next_t)


CHUNKS = 2


def body(traces, live):
    seg_dev, block, samples = traces.shape
    bins = samples // 2
    groups = lax.axis_size("tm")
    group_width = bins // groups
    width = group_width // CHUNKS
    segments = seg_dev * groups
    table = forward_table(samples, bins, group_width)
    inverse = inverse_table(samples, bins, group_width, segments).reshape(
        groups, 2, CHUNKS, width, samples
    )
    spectra = jnp.einsum("jat,tc->cja", traces, table, preferred_element_type=jnp.float32)
    flags = live.astype(jnp.float32)
    white = (whiten_cols(spectra, groups) * flags).astype(jnp.bfloat16)
    white = white.reshape(groups, 2, CHUNKS, width, seg_dev, block)
    lagged = None
    for chunk in range(CHUNKS):
        piece = white[:, :, chunk].reshape(groups * 2 * width, seg_dev, block)
        own = lax.all_to_all(piece, "tm", split_axis=0, concat_axis=1, tiled=True)
        own_t = jnp.swapaxes(own, 1, 2).reshape(2, width, block, segments)
        next_t = from_behind(own_t, "chan", -1)
        stack = cross(own_t, next_t).reshape(2 * width, block, block)
        gathered = lax.all_to_all(stack, "tm", split_axis=1, concat_axis=0, tiled=True)
        rows = inverse[:, :, chunk].reshape(groups * 2 * width, samples)
        part = jnp.einsum("hak,hl->akl", gathered, rows, preferred_element_type=jnp.float32)
        lagged = part if lagged is None else lagged + part
    return lagged.astype(jnp.bfloat16)


def solution(mesh):
    in_specs = (P("tm", "chan", None), P("chan"))
    out_specs = P(("chan", "tm"), None, None)
    return jax.shard_map(body, mesh=mesh, in_specs=in_specs, out_specs=out_specs, check_vma=False)
```

```python
import math

import jax
import jax.numpy as jnp
import numpy as np
from jax import lax
from jax.experimental import pallas as pl
from jax.experimental.pallas import tpu as pltpu
from jax.sharding import PartitionSpec as P

SMOOTH = 4


def from_behind(block, axis, distance):
    devices = range(lax.axis_size(axis))
    route = [(i - distance, i) for i in devices if i - distance in devices]
    return lax.ppermute(block, axis, route)


def column_bins(count, group_width):
    index = np.arange(count, dtype=np.int64)
    group = index // (2 * group_width)
    within = index % group_width
    is_imag = index // group_width % 2
    return (group * group_width + within, is_imag)


def angle_parts(freq, is_imag, steps, samples):
    phase = (steps[:, None] * freq[None, :] % samples).astype(np.float32) * np.float32(
        2.0 * math.pi / samples
    )
    phase = phase.astype(np.float64)
    cos_part, sin_part = np.cos(phase), np.sin(phase)
    lead = np.where(is_imag[None, :] == 1, -sin_part, cos_part)
    other = np.where(is_imag[None, :] == 1, cos_part, sin_part)
    return lead, other


def table_factors(samples, bins, group_width, segments, inner=128):
    freq, is_imag = column_bins(2 * bins, group_width)
    coarse = np.arange(samples // inner, dtype=np.int64) * inner
    fine = np.arange(inner, dtype=np.int64)
    lead, other = angle_parts(freq, is_imag, coarse, samples)
    fine_cos, fine_sin = angle_parts(freq, np.zeros_like(is_imag), fine, samples)
    weight = np.where(freq == 0, 1.0, 2.0) / math.sqrt(samples * segments)
    sign = np.where(freq * (samples // 2) % samples == 0, 1.0, -1.0)
    parts = (lead, other, fine_cos, fine_sin, (sign * weight)[None, :])
    flat = np.concatenate([p.astype(np.float32).reshape(-1) for p in parts])
    flat = lax.optimization_barrier(jnp.asarray(flat))
    out, at = [], 0
    for p in parts:
        out.append(flat[at : at + p.size].reshape(p.shape))
        at += p.size
    return out


def build_table(lead, other, fine_cos, fine_sin):
    table = lead[:, None, :] * fine_cos[None, :, :] - other[:, None, :] * fine_sin[None, :, :]
    return table.reshape(-1, lead.shape[-1]).astype(jnp.bfloat16)


def whiten_cols(spectra, groups):
    bins = spectra.shape[0] // 2
    width = bins // groups
    rest = spectra.shape[1:]
    split = spectra.reshape((groups, 2, width) + rest)
    real_part = split[:, 0].reshape((bins,) + rest)
    imag_part = split[:, 1].reshape((bins,) + rest)
    amplitude = jnp.sqrt(real_part * real_part + imag_part * imag_part)
    padded = jnp.pad(amplitude, [(SMOOTH, SMOOTH)] + [(0, 0)] * len(rest))
    smooth = sum((padded[i : i + bins] for i in range(2 * SMOOTH + 1))) / (2 * SMOOTH + 1)
    water = 0.8 * jnp.mean(amplitude, axis=0, keepdims=True) + 1e-06
    level = jnp.maximum(smooth, water).reshape((groups, 1, width) + rest)
    return (split / level).reshape(spectra.shape)


def cross_kernel(own_ref, next_ref, out_ref):
    block = own_ref.shape[2]
    row = lax.broadcasted_iota(jnp.int32, (block, block), 0)
    col = lax.broadcasted_iota(jnp.int32, (block, block), 1)
    flip = (row + col == block - 1).astype(jnp.bfloat16)

    def reverse_rows(x):
        return jnp.dot(flip, x, preferred_element_type=jnp.float32).astype(jnp.bfloat16)

    for f in range(own_ref.shape[1]):
        own_real = own_ref[0, f]
        own_imag = own_ref[1, f]
        own_both = jnp.concatenate([own_real, own_imag], axis=1)
        lhs = jnp.concatenate(
            [own_both, jnp.concatenate([own_imag, -own_real], axis=1)], axis=0
        )
        next_both = jnp.concatenate([next_ref[0, f], next_ref[1, f]], axis=1)
        rhs = jnp.concatenate([reverse_rows(next_both), reverse_rows(own_both)], axis=0)
        both = lax.dot_general(
            lhs, rhs, (((1,), (1,)), ((), ())), preferred_element_type=jnp.float32
        )
        for part in range(2):
            rows = both[part * block : (part + 1) * block]
            sheared = pltpu.roll(rows, 1, 1, stride=1, stride_axis=0)[:, block:]
            ordered = jnp.dot(
                sheared.astype(jnp.bfloat16), flip, preferred_element_type=jnp.float32
            )
            out_ref[part, f] = ordered.astype(out_ref.dtype)


def cross(own_t, next_t, interpret=False):
    two, width, block, segs = own_t.shape
    step = min(width, 8)
    spec = pl.BlockSpec((two, step, block, segs), lambda i: (0, i, 0, 0))
    return pl.pallas_call(
        cross_kernel,
        grid=(width // step,),
        in_specs=[spec, spec],
        out_specs=pl.BlockSpec((two, step, block, block), lambda i: (0, i, 0, 0)),
        out_shape=jax.ShapeDtypeStruct((two, width, block, block), jnp.bfloat16),
        interpret=interpret,
    )(own_t, next_t)


CHUNKS = 2


def body(traces, live):
    seg_dev, block, samples = traces.shape
    bins = samples // 2
    groups = lax.axis_size("tm")
    group_width = bins // groups
    width = group_width // CHUNKS
    segments = seg_dev * groups
    lead, other, fine_cos, fine_sin, scale = table_factors(samples, bins, group_width, segments)
    table = build_table(lead, other, fine_cos, fine_sin)
    columns = lambda x, chunk: x.reshape(-1, groups, 2, CHUNKS, width)[:, :, :, chunk].reshape(
        x.shape[0], -1
    )
    spectra = jnp.einsum("jat,tc->cja", traces, table, preferred_element_type=jnp.float32)
    flags = live.astype(jnp.float32)
    white = (whiten_cols(spectra, groups) * flags).astype(jnp.bfloat16)
    white = white.reshape(groups, 2, CHUNKS, width, seg_dev, block)
    lagged = None
    for chunk in range(CHUNKS):
        piece = white[:, :, chunk].reshape(groups * 2 * width, seg_dev, block)
        own = lax.all_to_all(piece, "tm", split_axis=0, concat_axis=1, tiled=True)
        own_t = jnp.swapaxes(own, 1, 2).reshape(2, width, block, segments)
        next_t = from_behind(own_t, "chan", -1)
        stack = cross(own_t, next_t).reshape(2 * width, block, block)
        gathered = lax.all_to_all(stack, "tm", split_axis=1, concat_axis=0, tiled=True)
        rows = build_table(
            columns(lead * scale, chunk),
            columns(other * scale, chunk),
            columns(fine_cos, chunk),
            columns(fine_sin, chunk),
        )
        part = jnp.einsum("hak,lh->akl", gathered, rows, preferred_element_type=jnp.float32)
        lagged = part if lagged is None else lagged + part
    return lagged.astype(jnp.bfloat16)


def solution(mesh):
    in_specs = (P("tm", "chan", None), P("chan"))
    out_specs = P(("chan", "tm"), None, None)
    return jax.shard_map(body, mesh=mesh, in_specs=in_specs, out_specs=out_specs, check_vma=False)
```

```python
import math

import jax
import jax.numpy as jnp
import numpy as np
from jax import lax
from jax.experimental import pallas as pl
from jax.experimental.pallas import tpu as pltpu
from jax.sharding import PartitionSpec as P

SMOOTH = 4


def from_behind(block, axis, distance):
    devices = range(lax.axis_size(axis))
    route = [(i - distance, i) for i in devices if i - distance in devices]
    return lax.ppermute(block, axis, route)


def column_bins(count, group_width):
    index = np.arange(count, dtype=np.int64)
    group = index // (2 * group_width)
    within = index % group_width
    is_imag = index // group_width % 2
    return (group * group_width + within, is_imag)


def forward_table(samples, bins, group_width):
    freq, is_imag = column_bins(2 * bins, group_width)
    moments = np.arange(samples, dtype=np.int64)[:, None]
    phase = (moments * freq[None, :] % samples).astype(np.float32) * np.float32(2.0 * math.pi / samples)
    phase = phase.astype(np.float64)
    table = np.where(is_imag[None, :] == 1, -np.sin(phase), np.cos(phase)).astype(np.float32)
    return jnp.asarray(table.astype(jnp.bfloat16))


def inverse_table(samples, bins, group_width, segments):
    freq, is_imag = column_bins(2 * bins, group_width)
    lag = np.arange(samples, dtype=np.int64) - samples // 2
    phase = np.mod(freq[:, None] * lag[None, :], samples).astype(np.float32) * np.float32(
        2.0 * math.pi / samples
    )
    phase = phase.astype(np.float64)
    weight = np.where(freq == 0, 1.0, 2.0).astype(np.float32) / np.float32(math.sqrt(samples * segments))
    wave = np.where(is_imag[:, None] == 1, -np.sin(phase), np.cos(phase)).astype(np.float32)
    return jnp.asarray((weight[:, None] * wave).astype(np.float32).astype(jnp.bfloat16))


def whiten_cols(spectra, groups):
    bins = spectra.shape[0] // 2
    width = bins // groups
    rest = spectra.shape[1:]
    split = spectra.reshape((groups, 2, width) + rest)
    real_part = split[:, 0].reshape((bins,) + rest)
    imag_part = split[:, 1].reshape((bins,) + rest)
    amplitude = jnp.sqrt(real_part * real_part + imag_part * imag_part)
    padded = jnp.pad(amplitude, [(SMOOTH, SMOOTH)] + [(0, 0)] * len(rest))
    smooth = sum((padded[i : i + bins] for i in range(2 * SMOOTH + 1))) / (2 * SMOOTH + 1)
    water = 0.8 * jnp.mean(amplitude, axis=0, keepdims=True) + 1e-06
    level = jnp.maximum(smooth, water).reshape((groups, 1, width) + rest)
    return (split / level).reshape(spectra.shape)


def cross_kernel(own_ref, next_ref, out_ref):
    block = own_ref.shape[2]
    row = lax.broadcasted_iota(jnp.int32, (block, block), 0)
    col = lax.broadcasted_iota(jnp.int32, (block, block), 1)
    flip = (row + col == block - 1).astype(jnp.bfloat16)

    def reverse_rows(x):
        return jnp.dot(flip, x, preferred_element_type=jnp.float32).astype(jnp.bfloat16)

    for f in range(own_ref.shape[1]):
        own_real = own_ref[0, f]
        own_imag = own_ref[1, f]
        own_both = jnp.concatenate([own_real, own_imag], axis=1)
        lhs = jnp.concatenate(
            [own_both, jnp.concatenate([own_imag, -own_real], axis=1)], axis=0
        )
        next_both = jnp.concatenate([next_ref[0, f], next_ref[1, f]], axis=1)
        rhs = jnp.concatenate([reverse_rows(next_both), reverse_rows(own_both)], axis=0)
        both = lax.dot_general(
            lhs, rhs, (((1,), (1,)), ((), ())), preferred_element_type=jnp.float32
        )
        for part in range(2):
            rows = both[part * block : (part + 1) * block]
            sheared = pltpu.roll(rows, 1, 1, stride=1, stride_axis=0)[:, block:]
            ordered = jnp.dot(
                sheared.astype(jnp.bfloat16), flip, preferred_element_type=jnp.float32
            )
            out_ref[part, f] = ordered.astype(out_ref.dtype)


def cross(own_t, next_t, interpret=False):
    two, width, block, segs = own_t.shape
    step = min(width, 8)
    spec = pl.BlockSpec((two, step, block, segs), lambda i: (0, i, 0, 0))
    return pl.pallas_call(
        cross_kernel,
        grid=(width // step,),
        in_specs=[spec, spec],
        out_specs=pl.BlockSpec((two, step, block, block), lambda i: (0, i, 0, 0)),
        out_shape=jax.ShapeDtypeStruct((two, width, block, block), jnp.bfloat16),
        interpret=interpret,
    )(own_t, next_t)


CHUNKS = 4


def body(traces, live):
    seg_dev, block, samples = traces.shape
    bins = samples // 2
    groups = lax.axis_size("tm")
    group_width = bins // groups
    width = group_width // CHUNKS
    segments = seg_dev * groups
    table = forward_table(samples, bins, group_width)
    inverse = inverse_table(samples, bins, group_width, segments).reshape(
        groups, 2, CHUNKS, width, samples
    )
    spectra = jnp.einsum("jat,tc->cja", traces, table, preferred_element_type=jnp.float32)
    flags = live.astype(jnp.float32)
    white = (whiten_cols(spectra, groups) * flags).astype(jnp.bfloat16)
    white = white.reshape(groups, 2, CHUNKS, width, seg_dev, block)
    lagged = None
    for chunk in range(CHUNKS):
        piece = white[:, :, chunk].reshape(groups * 2 * width, seg_dev, block)
        own = lax.all_to_all(piece, "tm", split_axis=0, concat_axis=1, tiled=True)
        own_t = jnp.swapaxes(own, 1, 2).reshape(2, width, block, segments)
        next_t = from_behind(own_t, "chan", -1)
        stack = cross(own_t, next_t).reshape(2 * width, block, block)
        gathered = lax.all_to_all(stack, "tm", split_axis=1, concat_axis=0, tiled=True)
        rows = inverse[:, :, chunk].reshape(groups * 2 * width, samples)
        part = jnp.einsum("hak,hl->akl", gathered, rows, preferred_element_type=jnp.float32)
        lagged = part if lagged is None else lagged + part
    return lagged.astype(jnp.bfloat16)


def solution(mesh):
    in_specs = (P("tm", "chan", None), P("chan"))
    out_specs = P(("chan", "tm"), None, None)
    return jax.shard_map(body, mesh=mesh, in_specs=in_specs, out_specs=out_specs, check_vma=False)
```

```python
import math

import jax
import jax.numpy as jnp
import numpy as np
from jax import lax
from jax.experimental import pallas as pl
from jax.experimental.pallas import tpu as pltpu
from jax.sharding import PartitionSpec as P

SMOOTH = 4


def from_behind(block, axis, distance):
    devices = range(lax.axis_size(axis))
    route = [(i - distance, i) for i in devices if i - distance in devices]
    return lax.ppermute(block, axis, route)


def column_bins(count, group_width):
    index = np.arange(count, dtype=np.int64)
    group = index // (2 * group_width)
    within = index % group_width
    is_imag = index // group_width % 2
    return (group * group_width + within, is_imag)


def forward_table(samples, bins, group_width):
    freq, is_imag = column_bins(2 * bins, group_width)
    moments = np.arange(samples, dtype=np.int64)[:, None]
    phase = (moments * freq[None, :] % samples).astype(np.float32) * np.float32(2.0 * math.pi / samples)
    phase = phase.astype(np.float64)
    table = np.where(is_imag[None, :] == 1, -np.sin(phase), np.cos(phase)).astype(np.float32)
    return jnp.asarray(table.astype(jnp.bfloat16))


def inverse_table(samples, bins, group_width, segments):
    freq, is_imag = column_bins(2 * bins, group_width)
    lag = np.arange(samples, dtype=np.int64) - samples // 2
    phase = np.mod(freq[:, None] * lag[None, :], samples).astype(np.float32) * np.float32(
        2.0 * math.pi / samples
    )
    phase = phase.astype(np.float64)
    weight = np.where(freq == 0, 1.0, 2.0).astype(np.float32) / np.float32(math.sqrt(samples * segments))
    wave = np.where(is_imag[:, None] == 1, -np.sin(phase), np.cos(phase)).astype(np.float32)
    return jnp.asarray((weight[:, None] * wave).astype(np.float32).astype(jnp.bfloat16))


def whiten_cols(spectra, groups):
    bins = spectra.shape[0] // 2
    width = bins // groups
    rest = spectra.shape[1:]
    split = spectra.reshape((groups, 2, width) + rest)
    real_part = split[:, 0].reshape((bins,) + rest)
    imag_part = split[:, 1].reshape((bins,) + rest)
    amplitude = jnp.sqrt(real_part * real_part + imag_part * imag_part)
    padded = jnp.pad(amplitude, [(SMOOTH, SMOOTH)] + [(0, 0)] * len(rest))
    smooth = sum((padded[i : i + bins] for i in range(2 * SMOOTH + 1))) / (2 * SMOOTH + 1)
    water = 0.8 * jnp.mean(amplitude, axis=0, keepdims=True) + 1e-06
    level = jnp.maximum(smooth, water).reshape((groups, 1, width) + rest)
    return (split / level).reshape(spectra.shape)


def cross_kernel(own_ref, next_ref, out_ref):
    block = own_ref.shape[2]
    row = lax.broadcasted_iota(jnp.int32, (block, block), 0)
    col = lax.broadcasted_iota(jnp.int32, (block, block), 1)
    flip = (row + col == block - 1).astype(jnp.bfloat16)

    def reverse_rows(x):
        return jnp.dot(flip, x, preferred_element_type=jnp.float32).astype(jnp.bfloat16)

    for f in range(own_ref.shape[1]):
        own_real = own_ref[0, f]
        own_imag = own_ref[1, f]
        own_both = jnp.concatenate([own_real, own_imag], axis=1)
        lhs = jnp.concatenate(
            [own_both, jnp.concatenate([own_imag, -own_real], axis=1)], axis=0
        )
        next_both = jnp.concatenate([next_ref[0, f], next_ref[1, f]], axis=1)
        rhs = jnp.concatenate([reverse_rows(next_both), reverse_rows(own_both)], axis=0)
        both = lax.dot_general(
            lhs, rhs, (((1,), (1,)), ((), ())), preferred_element_type=jnp.float32
        )
        for part in range(2):
            rows = both[part * block : (part + 1) * block]
            sheared = pltpu.roll(rows, 1, 1, stride=1, stride_axis=0)[:, block:]
            ordered = jnp.dot(
                sheared.astype(jnp.bfloat16), flip, preferred_element_type=jnp.float32
            )
            out_ref[part, f] = ordered.astype(out_ref.dtype)


def cross(own_t, next_t, interpret=False):
    two, width, block, segs = own_t.shape
    step = min(width, 8)
    spec = pl.BlockSpec((two, step, block, segs), lambda i: (0, i, 0, 0))
    return pl.pallas_call(
        cross_kernel,
        grid=(width // step,),
        in_specs=[spec, spec],
        out_specs=pl.BlockSpec((two, step, block, block), lambda i: (0, i, 0, 0)),
        out_shape=jax.ShapeDtypeStruct((two, width, block, block), jnp.bfloat16),
        interpret=interpret,
    )(own_t, next_t)


CHUNKS = 2
ROW = 4


def body(traces, live):
    seg_dev, block, samples = traces.shape
    bins = samples // 2
    groups = lax.axis_size("tm")
    group_width = bins // groups
    width = group_width // CHUNKS
    segments = seg_dev * groups
    table = forward_table(samples, bins, group_width)
    inverse = inverse_table(samples, bins, group_width, segments).reshape(
        groups, 2, CHUNKS, width, samples
    )
    spectra = jnp.einsum("jat,tc->cja", traces, table, preferred_element_type=jnp.float32)
    flags = live.astype(jnp.float32)
    white = (whiten_cols(spectra, groups) * flags).astype(jnp.bfloat16)
    white = white.reshape(groups, 2, CHUNKS, width, seg_dev, block)
    blocks = lax.axis_size("chan")
    inner_route = [(i + 1, i) for i in range(blocks - 1) if (i + 1) % ROW != 0]
    wrap_route = [(i + 1, i) for i in range(blocks - 1) if (i + 1) % ROW == 0]
    owns = []
    for chunk in range(CHUNKS):
        piece = white[:, :, chunk].reshape(groups * 2 * width, seg_dev, block)
        own = lax.all_to_all(piece, "tm", split_axis=0, concat_axis=1, tiled=True)
        owns.append(jnp.swapaxes(own, 1, 2).reshape(2, width, block, segments))
    lagged = None
    for chunk in range(CHUNKS):
        own_t = owns[chunk]
        gated, _ = lax.optimization_barrier((own_t, owns[-1]))
        next_t = lax.ppermute(own_t, "chan", inner_route) + lax.ppermute(gated, "chan", wrap_route)
        stack = cross(own_t, next_t).reshape(2 * width, block, block)
        gathered = lax.all_to_all(stack, "tm", split_axis=1, concat_axis=0, tiled=True)
        rows = inverse[:, :, chunk].reshape(groups * 2 * width, samples)
        part = jnp.einsum("hak,hl->akl", gathered, rows, preferred_element_type=jnp.float32)
        lagged = part if lagged is None else lagged + part
    return lagged.astype(jnp.bfloat16)


def solution(mesh):
    in_specs = (P("tm", "chan", None), P("chan"))
    out_specs = P(("chan", "tm"), None, None)
    return jax.shard_map(body, mesh=mesh, in_specs=in_specs, out_specs=out_specs, check_vma=False)
```

```python
import math

import jax
import jax.numpy as jnp
import numpy as np
from jax import lax
from jax.experimental import pallas as pl
from jax.experimental.pallas import tpu as pltpu
from jax.sharding import PartitionSpec as P

SMOOTH = 4


def from_behind(block, axis, distance):
    devices = range(lax.axis_size(axis))
    route = [(i - distance, i) for i in devices if i - distance in devices]
    return lax.ppermute(block, axis, route)


def column_bins(count, group_width):
    index = np.arange(count, dtype=np.int64)
    group = index // (2 * group_width)
    within = index % group_width
    is_imag = index // group_width % 2
    return (group * group_width + within, is_imag)


def forward_table(samples, bins, group_width):
    freq, is_imag = column_bins(2 * bins, group_width)
    moments = np.arange(samples, dtype=np.int64)[:, None]
    phase = (moments * freq[None, :] % samples).astype(np.float32) * np.float32(2.0 * math.pi / samples)
    phase = phase.astype(np.float64)
    table = np.where(is_imag[None, :] == 1, -np.sin(phase), np.cos(phase)).astype(np.float32)
    return jnp.asarray(table.astype(jnp.bfloat16))


def inverse_table(samples, bins, group_width, segments):
    freq, is_imag = column_bins(2 * bins, group_width)
    lag = np.arange(samples, dtype=np.int64) - samples // 2
    phase = np.mod(freq[:, None] * lag[None, :], samples).astype(np.float32) * np.float32(
        2.0 * math.pi / samples
    )
    phase = phase.astype(np.float64)
    weight = np.where(freq == 0, 1.0, 2.0).astype(np.float32) / np.float32(math.sqrt(samples * segments))
    wave = np.where(is_imag[:, None] == 1, -np.sin(phase), np.cos(phase)).astype(np.float32)
    return jnp.asarray((weight[:, None] * wave).astype(np.float32).astype(jnp.bfloat16))


def whiten_cols(spectra, groups):
    bins = spectra.shape[0] // 2
    width = bins // groups
    rest = spectra.shape[1:]
    split = spectra.reshape((groups, 2, width) + rest)
    real_part = split[:, 0].reshape((bins,) + rest)
    imag_part = split[:, 1].reshape((bins,) + rest)
    amplitude = jnp.sqrt(real_part * real_part + imag_part * imag_part)
    padded = jnp.pad(amplitude, [(SMOOTH, SMOOTH)] + [(0, 0)] * len(rest))
    smooth = sum((padded[i : i + bins] for i in range(2 * SMOOTH + 1))) / (2 * SMOOTH + 1)
    water = 0.8 * jnp.mean(amplitude, axis=0, keepdims=True) + 1e-06
    level = jnp.maximum(smooth, water).reshape((groups, 1, width) + rest)
    return (split / level).reshape(spectra.shape)


def cross_kernel(own_ref, next_ref, out_ref):
    block = own_ref.shape[2]
    row = lax.broadcasted_iota(jnp.int32, (block, block), 0)
    col = lax.broadcasted_iota(jnp.int32, (block, block), 1)
    flip = (row + col == block - 1).astype(jnp.bfloat16)

    def reverse_rows(x):
        return jnp.dot(flip, x, preferred_element_type=jnp.float32).astype(jnp.bfloat16)

    for f in range(own_ref.shape[1]):
        own_real = own_ref[0, f]
        own_imag = own_ref[1, f]
        own_both = jnp.concatenate([own_real, own_imag], axis=1)
        lhs = jnp.concatenate(
            [own_both, jnp.concatenate([own_imag, -own_real], axis=1)], axis=0
        )
        next_both = jnp.concatenate([next_ref[0, f], next_ref[1, f]], axis=1)
        rhs = jnp.concatenate([reverse_rows(next_both), reverse_rows(own_both)], axis=0)
        both = lax.dot_general(
            lhs, rhs, (((1,), (1,)), ((), ())), preferred_element_type=jnp.float32
        )
        for part in range(2):
            rows = both[part * block : (part + 1) * block]
            sheared = pltpu.roll(rows, 1, 1, stride=1, stride_axis=0)[:, block:]
            ordered = jnp.dot(
                sheared.astype(jnp.bfloat16), flip, preferred_element_type=jnp.float32
            )
            out_ref[part, f] = ordered.astype(out_ref.dtype)


def cross(own_t, next_t, interpret=False):
    two, width, block, segs = own_t.shape
    step = min(width, 8)
    spec = pl.BlockSpec((two, step, block, segs), lambda i: (0, i, 0, 0))
    return pl.pallas_call(
        cross_kernel,
        grid=(width // step,),
        in_specs=[spec, spec],
        out_specs=pl.BlockSpec((two, step, block, block), lambda i: (0, i, 0, 0)),
        out_shape=jax.ShapeDtypeStruct((two, width, block, block), jnp.bfloat16),
        interpret=interpret,
    )(own_t, next_t)


CHUNKS = 2
ROW = 4


def body(traces, live):
    seg_dev, block, samples = traces.shape
    bins = samples // 2
    groups = lax.axis_size("tm")
    group_width = bins // groups
    width = group_width // CHUNKS
    segments = seg_dev * groups
    table = forward_table(samples, bins, group_width)
    inverse = inverse_table(samples, bins, group_width, segments).reshape(
        groups, 2, CHUNKS, width, samples
    )
    spectra = jnp.einsum("jat,tc->cja", traces, table, preferred_element_type=jnp.float32)
    flags = live.astype(jnp.float32)
    white = (whiten_cols(spectra, groups) * flags).astype(jnp.bfloat16)
    white = white.reshape(groups, 2, CHUNKS, width, seg_dev, block)
    blocks = lax.axis_size("chan")
    inner_route = [(i + 1, i) for i in range(blocks - 1) if (i + 1) % ROW != 0]
    wrap_route = [(i + 1, i) for i in range(blocks - 1) if (i + 1) % ROW == 0]
    owns = []
    for chunk in range(CHUNKS):
        piece = white[:, :, chunk].reshape(groups * 2 * width, seg_dev, block)
        own = lax.all_to_all(piece, "tm", split_axis=0, concat_axis=1, tiled=True)
        owns.append(jnp.swapaxes(own, 1, 2).reshape(2, width, block, segments))
    lagged = None
    for chunk in range(CHUNKS):
        own_t = owns[chunk]
        if chunk == CHUNKS - 1:
            next_t = from_behind(own_t, "chan", -1)
        else:
            gated, _ = lax.optimization_barrier((own_t, owns[-1]))
            inner = lax.ppermute(own_t, "chan", inner_route)
            next_t = inner + lax.ppermute(gated, "chan", wrap_route)
        stack = cross(own_t, next_t).reshape(2 * width, block, block)
        gathered = lax.all_to_all(stack, "tm", split_axis=1, concat_axis=0, tiled=True)
        rows = inverse[:, :, chunk].reshape(groups * 2 * width, samples)
        part = jnp.einsum("hak,hl->akl", gathered, rows, preferred_element_type=jnp.float32)
        lagged = part if lagged is None else lagged + part
    return lagged.astype(jnp.bfloat16)


def solution(mesh):
    in_specs = (P("tm", "chan", None), P("chan"))
    out_specs = P(("chan", "tm"), None, None)

    return jax.shard_map(body, mesh=mesh, in_specs=in_specs, out_specs=out_specs, check_vma=False)
```

```python
import math

import jax
import jax.numpy as jnp
import numpy as np
from jax import lax
from jax.experimental import pallas as pl
from jax.experimental.pallas import tpu as pltpu
from jax.sharding import PartitionSpec as P

SMOOTH = 4


def from_behind(block, axis, distance):
    devices = range(lax.axis_size(axis))
    route = [(i - distance, i) for i in devices if i - distance in devices]
    return lax.ppermute(block, axis, route)


def column_bins(count, group_width):
    index = np.arange(count, dtype=np.int64)
    group = index // (2 * group_width)
    within = index % group_width
    is_imag = index // group_width % 2
    return (group * group_width + within, is_imag)


def forward_table(samples, bins, group_width):
    freq, is_imag = column_bins(2 * bins, group_width)
    moments = np.arange(samples, dtype=np.int64)[:, None]
    phase = (moments * freq[None, :] % samples).astype(np.float32) * np.float32(2.0 * math.pi / samples)
    phase = phase.astype(np.float64)
    table = np.where(is_imag[None, :] == 1, -np.sin(phase), np.cos(phase)).astype(np.float32)
    return jnp.asarray(table.astype(jnp.bfloat16))


def inverse_table(samples, bins, group_width, segments):
    freq, is_imag = column_bins(2 * bins, group_width)
    lag = np.arange(samples, dtype=np.int64) - samples // 2
    phase = np.mod(freq[:, None] * lag[None, :], samples).astype(np.float32) * np.float32(
        2.0 * math.pi / samples
    )
    phase = phase.astype(np.float64)
    weight = np.where(freq == 0, 1.0, 2.0).astype(np.float32) / np.float32(math.sqrt(samples * segments))
    wave = np.where(is_imag[:, None] == 1, -np.sin(phase), np.cos(phase)).astype(np.float32)
    return jnp.asarray((weight[:, None] * wave).astype(np.float32).astype(jnp.bfloat16))


def whiten_cols(spectra, groups):
    bins = spectra.shape[0] // 2
    width = bins // groups
    rest = spectra.shape[1:]
    split = spectra.reshape((groups, 2, width) + rest)
    real_part = split[:, 0].reshape((bins,) + rest)
    imag_part = split[:, 1].reshape((bins,) + rest)
    amplitude = jnp.sqrt(real_part * real_part + imag_part * imag_part)
    padded = jnp.pad(amplitude, [(SMOOTH, SMOOTH)] + [(0, 0)] * len(rest))
    smooth = sum((padded[i : i + bins] for i in range(2 * SMOOTH + 1))) / (2 * SMOOTH + 1)
    water = 0.8 * jnp.mean(amplitude, axis=0, keepdims=True) + 1e-06
    level = jnp.maximum(smooth, water).reshape((groups, 1, width) + rest)
    return (split / level).reshape(spectra.shape)


def cross_kernel(own_ref, next_ref, out_ref):
    block = own_ref.shape[2]
    row = lax.broadcasted_iota(jnp.int32, (block, block), 0)
    col = lax.broadcasted_iota(jnp.int32, (block, block), 1)
    flip = (row + col == block - 1).astype(jnp.bfloat16)

    def reverse_rows(x):
        return jnp.dot(flip, x, preferred_element_type=jnp.float32).astype(jnp.bfloat16)

    for f in range(own_ref.shape[1]):
        own_real = own_ref[0, f]
        own_imag = own_ref[1, f]
        own_both = jnp.concatenate([own_real, own_imag], axis=1)
        lhs = jnp.concatenate(
            [own_both, jnp.concatenate([own_imag, -own_real], axis=1)], axis=0
        )
        next_both = jnp.concatenate([next_ref[0, f], next_ref[1, f]], axis=1)
        rhs = jnp.concatenate([reverse_rows(next_both), reverse_rows(own_both)], axis=0)
        both = lax.dot_general(
            lhs, rhs, (((1,), (1,)), ((), ())), preferred_element_type=jnp.float32
        )
        for part in range(2):
            rows = both[part * block : (part + 1) * block]
            sheared = pltpu.roll(rows, 1, 1, stride=1, stride_axis=0)[:, block:]
            ordered = jnp.dot(
                sheared.astype(jnp.bfloat16), flip, preferred_element_type=jnp.float32
            )
            out_ref[part, f] = ordered.astype(out_ref.dtype)


def cross(own_t, next_t, interpret=False):
    two, width, block, segs = own_t.shape
    step = min(width, 8)
    spec = pl.BlockSpec((two, step, block, segs), lambda i: (0, i, 0, 0))
    return pl.pallas_call(
        cross_kernel,
        grid=(width // step,),
        in_specs=[spec, spec],
        out_specs=pl.BlockSpec((two, step, block, block), lambda i: (0, i, 0, 0)),
        out_shape=jax.ShapeDtypeStruct((two, width, block, block), jnp.bfloat16),
        interpret=interpret,
    )(own_t, next_t)


CHUNKS = 2
ROW = 4


def body(traces, live):
    seg_dev, block, samples = traces.shape
    bins = samples // 2
    groups = lax.axis_size("tm")
    group_width = bins // groups
    width = group_width // CHUNKS
    segments = seg_dev * groups
    table = forward_table(samples, bins, group_width)
    inverse = inverse_table(samples, bins, group_width, segments).reshape(
        groups, 2, CHUNKS, width, samples
    )
    spectra = jnp.einsum("jat,tc->cja", traces, table, preferred_element_type=jnp.float32)
    flags = live.astype(jnp.float32)
    white = (whiten_cols(spectra, groups) * flags).astype(jnp.bfloat16)
    white = white.reshape(groups, 2, CHUNKS, width, seg_dev, block)
    blocks = lax.axis_size("chan")
    inner_route = [(i + 1, i) for i in range(blocks - 1) if (i + 1) % ROW != 0]
    wrap_route = [
        ((i + 1) * groups + m, i * groups + (m ^ 2))
        for i in range(blocks - 1)
        if (i + 1) % ROW == 0
        for m in range(groups)
    ]
    swapped = lax.axis_index("chan") < ROW

    def swap_pairs(x):
        split = x.reshape((groups // 4, 2, 2) + x.shape[1:])
        return jnp.where(swapped, split[:, ::-1], split).reshape(x.shape)

    lagged = None
    for chunk in range(CHUNKS):
        piece = swap_pairs(white[:, :, chunk]).reshape(groups * 2 * width, seg_dev, block)
        own = lax.all_to_all(piece, "tm", split_axis=0, concat_axis=1, tiled=True)
        own_t = jnp.swapaxes(own, 1, 2).reshape(2, width, block, segments)
        next_t = lax.ppermute(own_t, "chan", inner_route) + lax.ppermute(
            own_t, ("chan", "tm"), wrap_route
        )
        stack = cross(own_t, next_t).reshape(2 * width, block, block)
        gathered = lax.all_to_all(stack, "tm", split_axis=1, concat_axis=0, tiled=True)
        gathered = swap_pairs(gathered.reshape(groups, 2 * width, block // groups, block)).reshape(
            gathered.shape
        )
        rows = inverse[:, :, chunk].reshape(groups * 2 * width, samples)
        part = jnp.einsum("hak,hl->akl", gathered, rows, preferred_element_type=jnp.float32)
        lagged = part if lagged is None else lagged + part
    return lagged.astype(jnp.bfloat16)


def solution(mesh):
    in_specs = (P("tm", "chan", None), P("chan"))
    out_specs = P(("chan", "tm"), None, None)
    return jax.shard_map(body, mesh=mesh, in_specs=in_specs, out_specs=out_specs, check_vma=False)
```

```python
import math

import jax
import jax.numpy as jnp
import numpy as np
from jax import lax
from jax.experimental import pallas as pl
from jax.experimental.pallas import tpu as pltpu
from jax.sharding import PartitionSpec as P

SMOOTH = 4


def from_behind(block, axis, distance):
    devices = range(lax.axis_size(axis))
    route = [(i - distance, i) for i in devices if i - distance in devices]
    return lax.ppermute(block, axis, route)


def column_bins(count, group_width):
    index = np.arange(count, dtype=np.int64)
    group = index // (2 * group_width)
    within = index % group_width
    is_imag = index // group_width % 2
    return (group * group_width + within, is_imag)


def forward_table(samples, bins, group_width):
    freq, is_imag = column_bins(2 * bins, group_width)
    moments = np.arange(samples, dtype=np.int64)[:, None]
    phase = (moments * freq[None, :] % samples).astype(np.float32) * np.float32(2.0 * math.pi / samples)
    phase = phase.astype(np.float64)
    table = np.where(is_imag[None, :] == 1, -np.sin(phase), np.cos(phase)).astype(np.float32)
    return jnp.asarray(table.astype(jnp.bfloat16))


def inverse_table(samples, bins, group_width, segments):
    freq, is_imag = column_bins(2 * bins, group_width)
    lag = np.arange(samples, dtype=np.int64) - samples // 2
    phase = np.mod(freq[:, None] * lag[None, :], samples).astype(np.float32) * np.float32(
        2.0 * math.pi / samples
    )
    phase = phase.astype(np.float64)
    weight = np.where(freq == 0, 1.0, 2.0).astype(np.float32) / np.float32(math.sqrt(samples * segments))
    wave = np.where(is_imag[:, None] == 1, -np.sin(phase), np.cos(phase)).astype(np.float32)
    return jnp.asarray((weight[:, None] * wave).astype(np.float32).astype(jnp.bfloat16))


def whiten_cols(spectra, groups):
    bins = spectra.shape[0] // 2
    width = bins // groups
    rest = spectra.shape[1:]
    split = spectra.reshape((groups, 2, width) + rest)
    real_part = split[:, 0].reshape((bins,) + rest)
    imag_part = split[:, 1].reshape((bins,) + rest)
    amplitude = jnp.sqrt(real_part * real_part + imag_part * imag_part)
    padded = jnp.pad(amplitude, [(SMOOTH, SMOOTH)] + [(0, 0)] * len(rest))
    smooth = sum((padded[i : i + bins] for i in range(2 * SMOOTH + 1))) / (2 * SMOOTH + 1)
    water = 0.8 * jnp.mean(amplitude, axis=0, keepdims=True) + 1e-06
    level = jnp.maximum(smooth, water).reshape((groups, 1, width) + rest)
    return (split / level).reshape(spectra.shape)


def cross_kernel(own_ref, next_ref, wrap_ref, out_ref):
    block = own_ref.shape[2]
    row = lax.broadcasted_iota(jnp.int32, (block, block), 0)
    col = lax.broadcasted_iota(jnp.int32, (block, block), 1)
    flip = (row + col == block - 1).astype(jnp.bfloat16)

    def reverse_rows(x):
        return jnp.dot(flip, x, preferred_element_type=jnp.float32).astype(jnp.bfloat16)

    for f in range(own_ref.shape[1]):
        own_real = own_ref[0, f]
        own_imag = own_ref[1, f]
        own_both = jnp.concatenate([own_real, own_imag], axis=1)
        lhs = jnp.concatenate(
            [own_both, jnp.concatenate([own_imag, -own_real], axis=1)], axis=0
        )
        next_both = jnp.concatenate(
            [next_ref[0, f] + wrap_ref[0, f], next_ref[1, f] + wrap_ref[1, f]], axis=1
        )
        rhs = jnp.concatenate([reverse_rows(next_both), reverse_rows(own_both)], axis=0)
        both = lax.dot_general(
            lhs, rhs, (((1,), (1,)), ((), ())), preferred_element_type=jnp.float32
        )
        for part in range(2):
            rows = both[part * block : (part + 1) * block]
            sheared = pltpu.roll(rows, 1, 1, stride=1, stride_axis=0)[:, block:]
            ordered = jnp.dot(
                sheared.astype(jnp.bfloat16), flip, preferred_element_type=jnp.float32
            )
            out_ref[part, f] = ordered.astype(out_ref.dtype)


def cross(own_t, next_t, wrap_t, interpret=False):
    two, width, block, segs = own_t.shape
    step = min(width, 8)
    spec = pl.BlockSpec((two, step, block, segs), lambda i: (0, i, 0, 0))
    return pl.pallas_call(
        cross_kernel,
        grid=(width // step,),
        in_specs=[spec, spec, spec],
        out_specs=pl.BlockSpec((two, step, block, block), lambda i: (0, i, 0, 0)),
        out_shape=jax.ShapeDtypeStruct((two, width, block, block), jnp.bfloat16),
        interpret=interpret,
    )(own_t, next_t, wrap_t)


CHUNKS = 2
ROW = 4


def body(traces, live):
    seg_dev, block, samples = traces.shape
    bins = samples // 2
    groups = lax.axis_size("tm")
    group_width = bins // groups
    width = group_width // CHUNKS
    segments = seg_dev * groups
    table = forward_table(samples, bins, group_width)
    inverse = inverse_table(samples, bins, group_width, segments).reshape(
        groups, 2, CHUNKS, width, samples
    )
    spectra = jnp.einsum("jat,tc->cja", traces, table, preferred_element_type=jnp.float32)
    flags = live.astype(jnp.float32)
    white = (whiten_cols(spectra, groups) * flags).astype(jnp.bfloat16)
    white = white.reshape(groups, 2, CHUNKS, width, seg_dev, block)
    blocks = lax.axis_size("chan")
    inner_route = [(i + 1, i) for i in range(blocks - 1) if (i + 1) % ROW != 0]
    wrap_route = [
        ((i + 1) * groups + m, i * groups + (m ^ 2))
        for i in range(blocks - 1)
        if (i + 1) % ROW == 0
        for m in range(groups)
    ]
    swapped = lax.axis_index("chan") < ROW

    def swap_pairs(x):
        split = x.reshape((groups // 4, 2, 2) + x.shape[1:])
        return jnp.where(swapped, split[:, ::-1], split).reshape(x.shape)

    lagged = None
    for chunk in range(CHUNKS):
        piece = swap_pairs(white[:, :, chunk]).reshape(groups * 2 * width, seg_dev, block)
        own = lax.all_to_all(piece, "tm", split_axis=0, concat_axis=1, tiled=True)
        own_t = jnp.swapaxes(own, 1, 2).reshape(2, width, block, segments)
        next_t = lax.ppermute(own_t, "chan", inner_route)
        wrap_t = lax.ppermute(own_t, ("chan", "tm"), wrap_route)
        stack = cross(own_t, next_t, wrap_t).reshape(2 * width, block, block)
        gathered = lax.all_to_all(stack, "tm", split_axis=1, concat_axis=0, tiled=True)
        gathered = swap_pairs(gathered.reshape(groups, 2 * width, block // groups, block)).reshape(
            gathered.shape
        )
        rows = inverse[:, :, chunk].reshape(groups * 2 * width, samples)
        part = jnp.einsum("hak,hl->akl", gathered, rows, preferred_element_type=jnp.float32)
        lagged = part if lagged is None else lagged + part
    return lagged.astype(jnp.bfloat16)


def solution(mesh):
    in_specs = (P("tm", "chan", None), P("chan"))
    out_specs = P(("chan", "tm"), None, None)
    return jax.shard_map(body, mesh=mesh, in_specs=in_specs, out_specs=out_specs, check_vma=False)
```

```python
import math

import jax
import jax.numpy as jnp
import numpy as np
from jax import lax
from jax.experimental import pallas as pl
from jax.experimental.pallas import tpu as pltpu
from jax.sharding import PartitionSpec as P

SMOOTH = 4


def from_behind(block, axis, distance):
    devices = range(lax.axis_size(axis))
    route = [(i - distance, i) for i in devices if i - distance in devices]
    return lax.ppermute(block, axis, route)


def column_bins(count, group_width):
    index = np.arange(count, dtype=np.int64)
    group = index // (2 * group_width)
    within = index % group_width
    is_imag = index // group_width % 2
    return (group * group_width + within, is_imag)


def forward_table(samples, bins, group_width):
    freq, is_imag = column_bins(2 * bins, group_width)
    moments = np.arange(samples, dtype=np.int64)[:, None]
    phase = (moments * freq[None, :] % samples).astype(np.float32) * np.float32(2.0 * math.pi / samples)
    phase = phase.astype(np.float64)
    table = np.where(is_imag[None, :] == 1, -np.sin(phase), np.cos(phase)).astype(np.float32)
    return jnp.asarray(table.astype(jnp.bfloat16))


def inverse_table(samples, bins, group_width, segments):
    freq, is_imag = column_bins(2 * bins, group_width)
    lag = np.arange(samples, dtype=np.int64) - samples // 2
    phase = np.mod(freq[:, None] * lag[None, :], samples).astype(np.float32) * np.float32(
        2.0 * math.pi / samples
    )
    phase = phase.astype(np.float64)
    weight = np.where(freq == 0, 1.0, 2.0).astype(np.float32) / np.float32(math.sqrt(samples * segments))
    wave = np.where(is_imag[:, None] == 1, -np.sin(phase), np.cos(phase)).astype(np.float32)
    return jnp.asarray((weight[:, None] * wave).astype(np.float32).astype(jnp.bfloat16))


def whiten_cols(spectra, groups):
    bins = spectra.shape[0] // 2
    width = bins // groups
    rest = spectra.shape[1:]
    split = spectra.reshape((groups, 2, width) + rest)
    real_part = split[:, 0].reshape((bins,) + rest)
    imag_part = split[:, 1].reshape((bins,) + rest)
    amplitude = jnp.sqrt(real_part * real_part + imag_part * imag_part)
    padded = jnp.pad(amplitude, [(SMOOTH, SMOOTH)] + [(0, 0)] * len(rest))
    smooth = sum((padded[i : i + bins] for i in range(2 * SMOOTH + 1))) / (2 * SMOOTH + 1)
    water = 0.8 * jnp.mean(amplitude, axis=0, keepdims=True) + 1e-06
    level = jnp.maximum(smooth, water).reshape((groups, 1, width) + rest)
    return (split / level).reshape(spectra.shape)


def cross_kernel(own_ref, next_ref, wrap_ref, out_ref):
    block = own_ref.shape[2]
    row = lax.broadcasted_iota(jnp.int32, (block, block), 0)
    col = lax.broadcasted_iota(jnp.int32, (block, block), 1)
    flip = (row + col == block - 1).astype(jnp.bfloat16)

    def reverse_rows(x):
        return jnp.dot(flip, x, preferred_element_type=jnp.float32).astype(jnp.bfloat16)

    for f in range(own_ref.shape[1]):
        own_real = own_ref[0, f]
        own_imag = own_ref[1, f]
        own_both = jnp.concatenate([own_real, own_imag], axis=1)
        lhs = jnp.concatenate(
            [own_both, jnp.concatenate([own_imag, -own_real], axis=1)], axis=0
        )
        next_both = jnp.concatenate(
            [next_ref[0, f] + wrap_ref[0, f], next_ref[1, f] + wrap_ref[1, f]], axis=1
        )
        rhs = jnp.concatenate([reverse_rows(next_both), reverse_rows(own_both)], axis=0)
        both = lax.dot_general(
            lhs, rhs, (((1,), (1,)), ((), ())), preferred_element_type=jnp.float32
        )
        for part in range(2):
            rows = both[part * block : (part + 1) * block]
            sheared = pltpu.roll(rows, 1, 1, stride=1, stride_axis=0)[:, block:]
            ordered = jnp.dot(
                sheared.astype(jnp.bfloat16), flip, preferred_element_type=jnp.float32
            )
            out_ref[:, part, f] = ordered.reshape(out_ref.shape[0], -1, block).astype(out_ref.dtype)


def cross(own_t, next_t, wrap_t, parts, interpret=False):
    two, width, block, segs = own_t.shape
    step = min(width, 8)
    spec = pl.BlockSpec((two, step, block, segs), lambda i: (0, i, 0, 0))
    return pl.pallas_call(
        cross_kernel,
        grid=(width // step,),
        in_specs=[spec, spec, spec],
        out_specs=pl.BlockSpec(
            (parts, two, step, block // parts, block), lambda i: (0, 0, i, 0, 0)
        ),
        out_shape=jax.ShapeDtypeStruct((parts, two, width, block // parts, block), jnp.bfloat16),
        interpret=interpret,
    )(own_t, next_t, wrap_t)


CHUNKS = 2
ROW = 4


def body(traces, live):
    seg_dev, block, samples = traces.shape
    bins = samples // 2
    groups = lax.axis_size("tm")
    group_width = bins // groups
    width = group_width // CHUNKS
    segments = seg_dev * groups
    table = forward_table(samples, bins, group_width)
    inverse = inverse_table(samples, bins, group_width, segments).reshape(
        groups, 2, CHUNKS, width, samples
    )
    spectra = jnp.einsum("jat,tc->cja", traces, table, preferred_element_type=jnp.float32)
    flags = live.astype(jnp.float32)
    white = (whiten_cols(spectra, groups) * flags).astype(jnp.bfloat16)
    white = white.reshape(groups, 2, CHUNKS, width, seg_dev, block)
    blocks = lax.axis_size("chan")
    inner_route = [(i + 1, i) for i in range(blocks - 1) if (i + 1) % ROW != 0]
    wrap_route = [
        ((i + 1) * groups + m, i * groups + (m ^ 2))
        for i in range(blocks - 1)
        if (i + 1) % ROW == 0
        for m in range(groups)
    ]
    swapped = lax.axis_index("chan") < ROW

    def swap_pairs(x):
        split = x.reshape((groups // 4, 2, 2) + x.shape[1:])
        return jnp.where(swapped, split[:, ::-1], split).reshape(x.shape)

    lagged = None
    for chunk in range(CHUNKS):
        piece = swap_pairs(white[:, :, chunk]).reshape(groups * 2 * width, seg_dev, block)
        own = lax.all_to_all(piece, "tm", split_axis=0, concat_axis=1, tiled=True)
        own_t = jnp.swapaxes(own, 1, 2).reshape(2, width, block, segments)
        next_t = lax.ppermute(own_t, "chan", inner_route)
        wrap_t = lax.ppermute(own_t, ("chan", "tm"), wrap_route)
        stack = cross(own_t, next_t, wrap_t, groups)
        gathered = lax.all_to_all(stack, "tm", split_axis=0, concat_axis=0, tiled=True)
        gathered = swap_pairs(gathered).reshape(groups * 2 * width, block // groups, block)
        rows = inverse[:, :, chunk].reshape(groups * 2 * width, samples)
        part = jnp.einsum("hak,hl->akl", gathered, rows, preferred_element_type=jnp.float32)
        lagged = part if lagged is None else lagged + part
    return lagged.astype(jnp.bfloat16)


def solution(mesh):
    in_specs = (P("tm", "chan", None), P("chan"))
    out_specs = P(("chan", "tm"), None, None)
    return jax.shard_map(body, mesh=mesh, in_specs=in_specs, out_specs=out_specs, check_vma=False)
```

```python
import math

import jax
import jax.numpy as jnp
import numpy as np
from jax import lax
from jax.experimental import pallas as pl
from jax.experimental.pallas import tpu as pltpu
from jax.sharding import PartitionSpec as P

SMOOTH = 4


def from_behind(block, axis, distance):
    devices = range(lax.axis_size(axis))
    route = [(i - distance, i) for i in devices if i - distance in devices]
    return lax.ppermute(block, axis, route)


def column_bins(count, group_width):
    index = np.arange(count, dtype=np.int64)
    group = index // (2 * group_width)
    within = index % group_width
    is_imag = index // group_width % 2
    return (group * group_width + within, is_imag)


def forward_table(samples, bins, group_width):
    freq, is_imag = column_bins(2 * bins, group_width)
    moments = np.arange(samples, dtype=np.int64)[:, None]
    phase = (moments * freq[None, :] % samples).astype(np.float32) * np.float32(2.0 * math.pi / samples)
    phase = phase.astype(np.float64)
    table = np.where(is_imag[None, :] == 1, -np.sin(phase), np.cos(phase)).astype(np.float32)
    return jnp.asarray(table.astype(jnp.bfloat16))


def inverse_table(samples, bins, group_width, segments):
    freq, is_imag = column_bins(2 * bins, group_width)
    lag = np.arange(samples, dtype=np.int64) - samples // 2
    phase = np.mod(freq[:, None] * lag[None, :], samples).astype(np.float32) * np.float32(
        2.0 * math.pi / samples
    )
    phase = phase.astype(np.float64)
    weight = np.where(freq == 0, 1.0, 2.0).astype(np.float32) / np.float32(math.sqrt(samples * segments))
    wave = np.where(is_imag[:, None] == 1, -np.sin(phase), np.cos(phase)).astype(np.float32)
    return jnp.asarray((weight[:, None] * wave).astype(np.float32).astype(jnp.bfloat16))


def whiten_cols(spectra, groups):
    bins = spectra.shape[0] // 2
    width = bins // groups
    rest = spectra.shape[1:]
    split = spectra.reshape((groups, 2, width) + rest)
    real_part = split[:, 0].reshape((bins,) + rest)
    imag_part = split[:, 1].reshape((bins,) + rest)
    amplitude = jnp.sqrt(real_part * real_part + imag_part * imag_part)
    padded = jnp.pad(amplitude, [(SMOOTH, SMOOTH)] + [(0, 0)] * len(rest))
    smooth = sum((padded[i : i + bins] for i in range(2 * SMOOTH + 1))) / (2 * SMOOTH + 1)
    water = 0.8 * jnp.mean(amplitude, axis=0, keepdims=True) + 1e-06
    level = jnp.maximum(smooth, water).reshape((groups, 1, width) + rest)
    return (split / level).reshape(spectra.shape)


def cross_kernel(own_ref, next_ref, wrap_ref, out_ref):
    block = own_ref.shape[2]
    row = lax.broadcasted_iota(jnp.int32, (block, block), 0)
    col = lax.broadcasted_iota(jnp.int32, (block, block), 1)
    flip = (row + col == block - 1).astype(jnp.bfloat16)

    def reverse_rows(x):
        return jnp.dot(flip, x, preferred_element_type=jnp.float32).astype(jnp.bfloat16)

    for f in range(own_ref.shape[1]):
        own_real = own_ref[0, f]
        own_imag = own_ref[1, f]
        own_both = jnp.concatenate([own_real, own_imag], axis=1)
        lhs = jnp.concatenate(
            [own_both, jnp.concatenate([own_imag, -own_real], axis=1)], axis=0
        )
        next_both = jnp.concatenate(
            [next_ref[0, f] + wrap_ref[0, f], next_ref[1, f] + wrap_ref[1, f]], axis=1
        )
        rhs = jnp.concatenate([reverse_rows(next_both), reverse_rows(own_both)], axis=0)
        both = lax.dot_general(
            lhs, rhs, (((1,), (1,)), ((), ())), preferred_element_type=jnp.float32
        )
        for part in range(2):
            rows = both[part * block : (part + 1) * block]
            sheared = pltpu.roll(rows, 1, 1, stride=1, stride_axis=0)[:, block:]
            ordered = jnp.dot(
                sheared.astype(jnp.bfloat16), flip, preferred_element_type=jnp.float32
            )
            out_ref[:, part, f] = ordered.reshape(out_ref.shape[0], -1, block).astype(out_ref.dtype)


def cross(own_t, next_t, wrap_t, parts, interpret=False):
    two, width, block, segs = own_t.shape
    step = min(width, 8)
    spec = pl.BlockSpec((two, step, block, segs), lambda i: (0, i, 0, 0))
    return pl.pallas_call(
        cross_kernel,
        grid=(width // step,),
        in_specs=[spec, spec, spec],
        out_specs=pl.BlockSpec(
            (parts, two, step, block // parts, block), lambda i: (0, 0, i, 0, 0)
        ),
        out_shape=jax.ShapeDtypeStruct((parts, two, width, block // parts, block), jnp.bfloat16),
        interpret=interpret,
    )(own_t, next_t, wrap_t)


CHUNKS = 2
ROW = 4


def body(traces, live):
    seg_dev, block, samples = traces.shape
    bins = samples // 2
    groups = lax.axis_size("tm")
    group_width = bins // groups
    width = group_width // CHUNKS
    segments = seg_dev * groups
    table = forward_table(samples, bins, group_width)
    inverse = inverse_table(samples, bins, group_width, segments).reshape(
        groups, 2, CHUNKS, width, samples
    )
    spectra = jnp.einsum("jat,tc->cja", traces, table, preferred_element_type=jnp.float32)
    flags = live.astype(jnp.float32)
    white = (whiten_cols(spectra, groups) * flags).astype(jnp.bfloat16)
    white = white.reshape(groups, 2, CHUNKS, width, seg_dev, block)
    blocks = lax.axis_size("chan")
    inner_route = [(i + 1, i) for i in range(blocks - 1) if (i + 1) % ROW != 0]
    wrap_route = [
        ((i + 1) * groups + m, i * groups + (m ^ 2))
        for i in range(blocks - 1)
        if (i + 1) % ROW == 0
        for m in range(groups)
    ]
    swapped = lax.axis_index("chan") < ROW

    def swap_pairs(x):
        split = x.reshape((groups // 4, 2, 2) + x.shape[1:])
        return jnp.where(swapped, split[:, ::-1], split).reshape(x.shape)

    lagged = None
    for chunk in range(CHUNKS):
        piece = swap_pairs(white[:, :, chunk]).reshape(groups * 2 * width, seg_dev, block)
        own = lax.all_to_all(piece, "tm", split_axis=0, concat_axis=1, tiled=True)
        own_t = jnp.swapaxes(own, 1, 2).reshape(2, width, block, segments)
        next_t = lax.ppermute(own_t, "chan", inner_route)
        wrap_t = lax.ppermute(own_t, ("chan", "tm"), wrap_route)
        stack = cross(own_t, next_t, wrap_t, groups)
        gathered = lax.all_to_all(stack, "tm", split_axis=0, concat_axis=0, tiled=True)
        gathered = gathered.reshape(groups * 2 * width, block // groups, block)
        rows = swap_pairs(inverse[:, :, chunk]).reshape(groups * 2 * width, samples)
        part = jnp.einsum("hak,hl->akl", gathered, rows, preferred_element_type=jnp.float32)
        lagged = part if lagged is None else lagged + part
    return lagged.astype(jnp.bfloat16)


def solution(mesh):
    in_specs = (P("tm", "chan", None), P("chan"))
    out_specs = P(("chan", "tm"), None, None)
    return jax.shard_map(body, mesh=mesh, in_specs=in_specs, out_specs=out_specs, check_vma=False)
```

```python
import math

import jax
import jax.numpy as jnp
import numpy as np
from jax import lax
from jax.experimental import pallas as pl
from jax.experimental.pallas import tpu as pltpu
from jax.sharding import PartitionSpec as P

SMOOTH = 4


def from_behind(block, axis, distance):
    devices = range(lax.axis_size(axis))
    route = [(i - distance, i) for i in devices if i - distance in devices]
    return lax.ppermute(block, axis, route)


def column_bins(count, group_width):
    index = np.arange(count, dtype=np.int64)
    group = index // (2 * group_width)
    within = index % group_width
    is_imag = index // group_width % 2
    return (group * group_width + within, is_imag)


def forward_table(samples, bins, group_width):
    freq, is_imag = column_bins(2 * bins, group_width)
    moments = np.arange(samples, dtype=np.int64)[:, None]
    phase = (moments * freq[None, :] % samples).astype(np.float32) * np.float32(2.0 * math.pi / samples)
    phase = phase.astype(np.float64)
    table = np.where(is_imag[None, :] == 1, -np.sin(phase), np.cos(phase)).astype(np.float32)
    return jnp.asarray(table.astype(jnp.bfloat16))


def inverse_table(samples, bins, group_width, segments):
    freq, is_imag = column_bins(2 * bins, group_width)
    lag = np.arange(samples, dtype=np.int64) - samples // 2
    phase = np.mod(freq[:, None] * lag[None, :], samples).astype(np.float32) * np.float32(
        2.0 * math.pi / samples
    )
    phase = phase.astype(np.float64)
    weight = np.where(freq == 0, 1.0, 2.0).astype(np.float32) / np.float32(math.sqrt(samples * segments))
    wave = np.where(is_imag[:, None] == 1, -np.sin(phase), np.cos(phase)).astype(np.float32)
    return jnp.asarray((weight[:, None] * wave).astype(np.float32).astype(jnp.bfloat16))


def whiten_cols(spectra, groups):
    bins = spectra.shape[0] // 2
    width = bins // groups
    rest = spectra.shape[1:]
    split = spectra.reshape((groups, 2, width) + rest)
    real_part = split[:, 0].reshape((bins,) + rest)
    imag_part = split[:, 1].reshape((bins,) + rest)
    amplitude = jnp.sqrt(real_part * real_part + imag_part * imag_part)
    padded = jnp.pad(amplitude, [(SMOOTH, SMOOTH)] + [(0, 0)] * len(rest))
    triple = padded[: bins + 6] + padded[1 : bins + 7] + padded[2 : bins + 8]
    smooth = (triple[:bins] + triple[3 : bins + 3] + triple[6 : bins + 6]) / (2 * SMOOTH + 1)
    water = 0.8 * jnp.mean(amplitude, axis=0, keepdims=True) + 1e-06
    level = jnp.maximum(smooth, water).reshape((groups, 1, width) + rest)
    return (split / level).reshape(spectra.shape)


def cross_kernel(own_ref, next_ref, wrap_ref, out_ref):
    block = own_ref.shape[2]
    row = lax.broadcasted_iota(jnp.int32, (block, block), 0)
    col = lax.broadcasted_iota(jnp.int32, (block, block), 1)
    flip = (row + col == block - 1).astype(jnp.bfloat16)

    def reverse_rows(x):
        return jnp.dot(flip, x, preferred_element_type=jnp.float32).astype(jnp.bfloat16)

    for f in range(own_ref.shape[1]):
        own_real = own_ref[0, f]
        own_imag = own_ref[1, f]
        own_both = jnp.concatenate([own_real, own_imag], axis=1)
        lhs = jnp.concatenate(
            [own_both, jnp.concatenate([own_imag, -own_real], axis=1)], axis=0
        )
        next_both = jnp.concatenate(
            [next_ref[0, f] + wrap_ref[0, f], next_ref[1, f] + wrap_ref[1, f]], axis=1
        )
        rhs = jnp.concatenate([reverse_rows(next_both), reverse_rows(own_both)], axis=0)
        both = lax.dot_general(
            lhs, rhs, (((1,), (1,)), ((), ())), preferred_element_type=jnp.float32
        )
        for part in range(2):
            rows = both[part * block : (part + 1) * block]
            sheared = pltpu.roll(rows, 1, 1, stride=1, stride_axis=0)[:, block:]
            ordered = jnp.dot(
                sheared.astype(jnp.bfloat16), flip, preferred_element_type=jnp.float32
            )
            out_ref[:, part, f] = ordered.reshape(out_ref.shape[0], -1, block).astype(out_ref.dtype)


def cross(own_t, next_t, wrap_t, parts, interpret=False):
    two, width, block, segs = own_t.shape
    step = min(width, 8)
    spec = pl.BlockSpec((two, step, block, segs), lambda i: (0, i, 0, 0))
    return pl.pallas_call(
        cross_kernel,
        grid=(width // step,),
        in_specs=[spec, spec, spec],
        out_specs=pl.BlockSpec(
            (parts, two, step, block // parts, block), lambda i: (0, 0, i, 0, 0)
        ),
        out_shape=jax.ShapeDtypeStruct((parts, two, width, block // parts, block), jnp.bfloat16),
        interpret=interpret,
    )(own_t, next_t, wrap_t)


CHUNKS = 2
ROW = 4


def body(traces, live):
    seg_dev, block, samples = traces.shape
    bins = samples // 2
    groups = lax.axis_size("tm")
    group_width = bins // groups
    width = group_width // CHUNKS
    segments = seg_dev * groups
    table = forward_table(samples, bins, group_width)
    inverse = inverse_table(samples, bins, group_width, segments).reshape(
        groups, 2, CHUNKS, width, samples
    )
    spectra = jnp.einsum("jat,tc->cja", traces, table, preferred_element_type=jnp.float32)
    flags = live.astype(jnp.float32)
    white = (whiten_cols(spectra, groups) * flags).astype(jnp.bfloat16)
    white = white.reshape(groups, 2, CHUNKS, width, seg_dev, block)
    blocks = lax.axis_size("chan")
    inner_route = [(i + 1, i) for i in range(blocks - 1) if (i + 1) % ROW != 0]
    wrap_route = [
        ((i + 1) * groups + m, i * groups + (m ^ 2))
        for i in range(blocks - 1)
        if (i + 1) % ROW == 0
        for m in range(groups)
    ]
    swapped = lax.axis_index("chan") < ROW

    def swap_pairs(x):
        split = x.reshape((groups // 4, 2, 2) + x.shape[1:])
        return jnp.where(swapped, split[:, ::-1], split).reshape(x.shape)

    lagged = None
    for chunk in range(CHUNKS):
        piece = swap_pairs(white[:, :, chunk]).reshape(groups * 2 * width, seg_dev, block)
        own = lax.all_to_all(piece, "tm", split_axis=0, concat_axis=1, tiled=True)
        own_t = jnp.swapaxes(own, 1, 2).reshape(2, width, block, segments)
        next_t = lax.ppermute(own_t, "chan", inner_route)
        wrap_t = lax.ppermute(own_t, ("chan", "tm"), wrap_route)
        stack = cross(own_t, next_t, wrap_t, groups)
        gathered = lax.all_to_all(stack, "tm", split_axis=0, concat_axis=0, tiled=True)
        gathered = gathered.reshape(groups * 2 * width, block // groups, block)
        rows = swap_pairs(inverse[:, :, chunk]).reshape(groups * 2 * width, samples)
        part = jnp.einsum("hak,hl->akl", gathered, rows, preferred_element_type=jnp.float32)
        lagged = part if lagged is None else lagged + part
    return lagged.astype(jnp.bfloat16)


def solution(mesh):
    in_specs = (P("tm", "chan", None), P("chan"))
    out_specs = P(("chan", "tm"), None, None)
    return jax.shard_map(body, mesh=mesh, in_specs=in_specs, out_specs=out_specs, check_vma=False)
```

```python
import math

import jax
import jax.numpy as jnp
import numpy as np
from jax import lax
from jax.experimental import pallas as pl
from jax.experimental.pallas import tpu as pltpu
from jax.sharding import PartitionSpec as P

SMOOTH = 4


def from_behind(block, axis, distance):
    devices = range(lax.axis_size(axis))
    route = [(i - distance, i) for i in devices if i - distance in devices]
    return lax.ppermute(block, axis, route)


def column_bins(count, group_width):
    index = np.arange(count, dtype=np.int64)
    group = index // (2 * group_width)
    within = index % group_width
    is_imag = index // group_width % 2
    return (group * group_width + within, is_imag)


def forward_table(samples, bins, group_width):
    freq, is_imag = column_bins(2 * bins, group_width)
    moments = np.arange(samples, dtype=np.int64)[:, None]
    phase = (moments * freq[None, :] % samples).astype(np.float32) * np.float32(2.0 * math.pi / samples)
    phase = phase.astype(np.float64)
    table = np.where(is_imag[None, :] == 1, -np.sin(phase), np.cos(phase)).astype(np.float32)
    return jnp.asarray(table.astype(jnp.bfloat16))


def inverse_table(samples, bins, group_width, segments):
    freq, is_imag = column_bins(2 * bins, group_width)
    lag = np.arange(samples, dtype=np.int64) - samples // 2
    phase = np.mod(freq[:, None] * lag[None, :], samples).astype(np.float32) * np.float32(
        2.0 * math.pi / samples
    )
    phase = phase.astype(np.float64)
    weight = np.where(freq == 0, 1.0, 2.0).astype(np.float32) / np.float32(math.sqrt(samples * segments))
    wave = np.where(is_imag[:, None] == 1, -np.sin(phase), np.cos(phase)).astype(np.float32)
    return jnp.asarray((weight[:, None] * wave).astype(np.float32).astype(jnp.bfloat16))


def whiten_cols(spectra, groups):
    bins = spectra.shape[0] // 2
    width = bins // groups
    rest = spectra.shape[1:]
    split = spectra.reshape((groups, 2, width) + rest)
    real_part = split[:, 0].reshape((bins,) + rest)
    imag_part = split[:, 1].reshape((bins,) + rest)
    amplitude = jnp.sqrt(real_part * real_part + imag_part * imag_part)
    padded = jnp.pad(amplitude, [(SMOOTH, SMOOTH)] + [(0, 0)] * len(rest))
    triple = padded[: bins + 6] + padded[1 : bins + 7] + padded[2 : bins + 8]
    smooth = (triple[:bins] + triple[3 : bins + 3] + triple[6 : bins + 6]) / (2 * SMOOTH + 1)
    water = 0.8 * jnp.mean(amplitude, axis=0, keepdims=True) + 1e-06
    level = jnp.maximum(smooth, water).reshape((groups, 1, width) + rest)
    return (split / level).reshape(spectra.shape)


def cross_kernel(own_ref, next_ref, wrap_ref, out_ref):
    block = own_ref.shape[2]
    row = lax.broadcasted_iota(jnp.int32, (block, block), 0)
    col = lax.broadcasted_iota(jnp.int32, (block, block), 1)
    flip = (row + col == block - 1).astype(jnp.bfloat16)

    def reverse_rows(x):
        return jnp.dot(flip, x, preferred_element_type=jnp.float32).astype(jnp.bfloat16)

    for f in range(own_ref.shape[1]):
        own_real = own_ref[0, f]
        own_imag = own_ref[1, f]
        own_both = jnp.concatenate([own_real, own_imag], axis=1)
        lhs = jnp.concatenate(
            [own_both, jnp.concatenate([own_imag, -own_real], axis=1)], axis=0
        )
        next_both = jnp.concatenate(
            [next_ref[0, f] + wrap_ref[0, f], next_ref[1, f] + wrap_ref[1, f]], axis=1
        )
        rhs = jnp.concatenate([reverse_rows(next_both), reverse_rows(own_both)], axis=0)
        both = lax.dot_general(
            lhs, rhs, (((1,), (1,)), ((), ())), preferred_element_type=jnp.float32
        )
        for part in range(2):
            rows = both[part * block : (part + 1) * block]
            sheared = pltpu.roll(rows, 1, 1, stride=1, stride_axis=0)[:, block:]
            ordered = jnp.dot(
                sheared.astype(jnp.bfloat16), flip, preferred_element_type=jnp.float32
            )
            out_ref[:, part, f] = ordered.reshape(out_ref.shape[0], -1, block).astype(out_ref.dtype)


def cross(own_t, next_t, wrap_t, parts, interpret=False):
    two, width, block, segs = own_t.shape
    step = min(width, 8)
    spec = pl.BlockSpec((two, step, block, segs), lambda i: (0, i, 0, 0))
    return pl.pallas_call(
        cross_kernel,
        grid=(width // step,),
        in_specs=[spec, spec, spec],
        out_specs=pl.BlockSpec(
            (parts, two, step, block // parts, block), lambda i: (0, 0, i, 0, 0)
        ),
        out_shape=jax.ShapeDtypeStruct((parts, two, width, block // parts, block), jnp.bfloat16),
        interpret=interpret,
    )(own_t, next_t, wrap_t)


CHUNKS = 2
ROW = 4


def body(traces, live):
    seg_dev, block, samples = traces.shape
    bins = samples // 2
    groups = lax.axis_size("tm")
    group_width = bins // groups
    widths = (group_width * 5 // 8, group_width * 3 // 8)
    segments = seg_dev * groups
    table = forward_table(samples, bins, group_width)
    inverse = inverse_table(samples, bins, group_width, segments).reshape(
        groups, 2, group_width, samples
    )
    spectra = jnp.einsum("jat,tc->cja", traces, table, preferred_element_type=jnp.float32)
    flags = live.astype(jnp.float32)
    white = (whiten_cols(spectra, groups) * flags).astype(jnp.bfloat16)
    white = white.reshape(groups, 2, group_width, seg_dev, block)
    blocks = lax.axis_size("chan")
    inner_route = [(i + 1, i) for i in range(blocks - 1) if (i + 1) % ROW != 0]
    wrap_route = [
        ((i + 1) * groups + m, i * groups + (m ^ 2))
        for i in range(blocks - 1)
        if (i + 1) % ROW == 0
        for m in range(groups)
    ]
    swapped = lax.axis_index("chan") < ROW

    def swap_pairs(x):
        split = x.reshape((groups // 4, 2, 2) + x.shape[1:])
        return jnp.where(swapped, split[:, ::-1], split).reshape(x.shape)

    lagged = None
    for chunk, width in enumerate(widths):
        first = sum(widths[:chunk])
        piece = swap_pairs(white[:, :, first : first + width])
        piece = piece.reshape(groups * 2 * width, seg_dev, block)
        own = lax.all_to_all(piece, "tm", split_axis=0, concat_axis=1, tiled=True)
        own_t = jnp.swapaxes(own, 1, 2).reshape(2, width, block, segments)
        next_t = lax.ppermute(own_t, "chan", inner_route)
        wrap_t = lax.ppermute(own_t, ("chan", "tm"), wrap_route)
        stack = cross(own_t, next_t, wrap_t, groups)
        gathered = lax.all_to_all(stack, "tm", split_axis=0, concat_axis=0, tiled=True)
        gathered = gathered.reshape(groups * 2 * width, block // groups, block)
        rows = swap_pairs(inverse[:, :, first : first + width]).reshape(groups * 2 * width, samples)
        part = jnp.einsum("hak,hl->akl", gathered, rows, preferred_element_type=jnp.float32)
        lagged = part if lagged is None else lagged + part
    return lagged.astype(jnp.bfloat16)


def solution(mesh):
    in_specs = (P("tm", "chan", None), P("chan"))
    out_specs = P(("chan", "tm"), None, None)
    return jax.shard_map(body, mesh=mesh, in_specs=in_specs, out_specs=out_specs, check_vma=False)
```

```python
import math

import jax
import jax.numpy as jnp
import numpy as np
from jax import lax
from jax.experimental import pallas as pl
from jax.experimental.pallas import tpu as pltpu
from jax.sharding import PartitionSpec as P

SMOOTH = 4


def from_behind(block, axis, distance):
    devices = range(lax.axis_size(axis))
    route = [(i - distance, i) for i in devices if i - distance in devices]
    return lax.ppermute(block, axis, route)


def column_bins(count, group_width):
    index = np.arange(count, dtype=np.int64)
    group = index // (2 * group_width)
    within = index % group_width
    is_imag = index // group_width % 2
    return (group * group_width + within, is_imag)


def forward_table(samples, bins, group_width):
    freq, is_imag = column_bins(2 * bins, group_width)
    moments = np.arange(samples, dtype=np.int64)[:, None]
    phase = (moments * freq[None, :] % samples).astype(np.float32) * np.float32(2.0 * math.pi / samples)
    phase = phase.astype(np.float64)
    table = np.where(is_imag[None, :] == 1, -np.sin(phase), np.cos(phase)).astype(np.float32)
    return jnp.asarray(table.astype(jnp.bfloat16))


def inverse_table(samples, bins, group_width, segments):
    freq, is_imag = column_bins(2 * bins, group_width)
    lag = np.arange(samples, dtype=np.int64) - samples // 2
    phase = np.mod(freq[:, None] * lag[None, :], samples).astype(np.float32) * np.float32(
        2.0 * math.pi / samples
    )
    phase = phase.astype(np.float64)
    weight = np.where(freq == 0, 1.0, 2.0).astype(np.float32) / np.float32(math.sqrt(samples * segments))
    wave = np.where(is_imag[:, None] == 1, -np.sin(phase), np.cos(phase)).astype(np.float32)
    return jnp.asarray((weight[:, None] * wave).astype(np.float32).astype(jnp.bfloat16))


def whiten_cols(spectra, groups):
    bins = spectra.shape[0] // 2
    width = bins // groups
    rest = spectra.shape[1:]
    split = spectra.reshape((groups, 2, width) + rest)
    real_part = split[:, 0].reshape((bins,) + rest)
    imag_part = split[:, 1].reshape((bins,) + rest)
    amplitude = jnp.sqrt(real_part * real_part + imag_part * imag_part)
    padded = jnp.pad(amplitude, [(SMOOTH, SMOOTH)] + [(0, 0)] * len(rest))
    triple = padded[: bins + 6] + padded[1 : bins + 7] + padded[2 : bins + 8]
    smooth = (triple[:bins] + triple[3 : bins + 3] + triple[6 : bins + 6]) / (2 * SMOOTH + 1)
    water = 0.8 * jnp.mean(amplitude, axis=0, keepdims=True) + 1e-06
    level = jnp.maximum(smooth, water).reshape((groups, 1, width) + rest)
    return (split / level).reshape(spectra.shape)


def cross_kernel(own_ref, next_ref, wrap_ref, out_ref):
    block = own_ref.shape[2]
    row = lax.broadcasted_iota(jnp.int32, (block, block), 0)
    col = lax.broadcasted_iota(jnp.int32, (block, block), 1)
    flip = (row + col == block - 1).astype(jnp.bfloat16)

    def reverse_rows(x):
        return jnp.dot(flip, x, preferred_element_type=jnp.float32).astype(jnp.bfloat16)

    for f in range(own_ref.shape[1]):
        own_real = own_ref[0, f]
        own_imag = own_ref[1, f]
        own_both = jnp.concatenate([own_real, own_imag], axis=1)
        lhs = jnp.concatenate(
            [own_both, jnp.concatenate([own_imag, -own_real], axis=1)], axis=0
        )
        next_both = jnp.concatenate(
            [next_ref[0, f] + wrap_ref[0, f], next_ref[1, f] + wrap_ref[1, f]], axis=1
        )
        rhs = jnp.concatenate([reverse_rows(next_both), reverse_rows(own_both)], axis=0)
        both = lax.dot_general(
            lhs, rhs, (((1,), (1,)), ((), ())), preferred_element_type=jnp.float32
        )
        for part in range(2):
            rows = both[part * block : (part + 1) * block]
            sheared = pltpu.roll(rows, 1, 1, stride=1, stride_axis=0)[:, block:]
            ordered = jnp.dot(
                sheared.astype(jnp.bfloat16), flip, preferred_element_type=jnp.float32
            )
            out_ref[:, part, f] = ordered.reshape(out_ref.shape[0], -1, block).astype(out_ref.dtype)


def cross(own_t, next_t, wrap_t, parts, interpret=False):
    two, width, block, segs = own_t.shape
    step = min(width, 16)
    spec = pl.BlockSpec((two, step, block, segs), lambda i: (0, i, 0, 0))
    return pl.pallas_call(
        cross_kernel,
        grid=(width // step,),
        in_specs=[spec, spec, spec],
        out_specs=pl.BlockSpec(
            (parts, two, step, block // parts, block), lambda i: (0, 0, i, 0, 0)
        ),
        out_shape=jax.ShapeDtypeStruct((parts, two, width, block // parts, block), jnp.bfloat16),
        interpret=interpret,
    )(own_t, next_t, wrap_t)


CHUNKS = 2
ROW = 4


def body(traces, live):
    seg_dev, block, samples = traces.shape
    bins = samples // 2
    groups = lax.axis_size("tm")
    group_width = bins // groups
    width = group_width // CHUNKS
    segments = seg_dev * groups
    table = forward_table(samples, bins, group_width)
    inverse = inverse_table(samples, bins, group_width, segments).reshape(
        groups, 2, CHUNKS, width, samples
    )
    spectra = jnp.einsum("jat,tc->cja", traces, table, preferred_element_type=jnp.float32)
    flags = live.astype(jnp.float32)
    white = (whiten_cols(spectra, groups) * flags).astype(jnp.bfloat16)
    white = white.reshape(groups, 2, CHUNKS, width, seg_dev, block)
    blocks = lax.axis_size("chan")
    inner_route = [(i + 1, i) for i in range(blocks - 1) if (i + 1) % ROW != 0]
    wrap_route = [
        ((i + 1) * groups + m, i * groups + (m ^ 2))
        for i in range(blocks - 1)
        if (i + 1) % ROW == 0
        for m in range(groups)
    ]
    swapped = lax.axis_index("chan") < ROW

    def swap_pairs(x):
        split = x.reshape((groups // 4, 2, 2) + x.shape[1:])
        return jnp.where(swapped, split[:, ::-1], split).reshape(x.shape)

    lagged = None
    for chunk in range(CHUNKS):
        piece = swap_pairs(white[:, :, chunk]).reshape(groups * 2 * width, seg_dev, block)
        own = lax.all_to_all(piece, "tm", split_axis=0, concat_axis=1, tiled=True)
        own_t = jnp.swapaxes(own, 1, 2).reshape(2, width, block, segments)
        next_t = lax.ppermute(own_t, "chan", inner_route)
        wrap_t = lax.ppermute(own_t, ("chan", "tm"), wrap_route)
        stack = cross(own_t, next_t, wrap_t, groups)
        gathered = lax.all_to_all(stack, "tm", split_axis=0, concat_axis=0, tiled=True)
        gathered = gathered.reshape(groups * 2 * width, block // groups, block)
        rows = swap_pairs(inverse[:, :, chunk]).reshape(groups * 2 * width, samples)
        part = jnp.einsum("hak,hl->akl", gathered, rows, preferred_element_type=jnp.float32)
        lagged = part if lagged is None else lagged + part
    return lagged.astype(jnp.bfloat16)


def solution(mesh):
    in_specs = (P("tm", "chan", None), P("chan"))
    out_specs = P(("chan", "tm"), None, None)
    return jax.shard_map(body, mesh=mesh, in_specs=in_specs, out_specs=out_specs, check_vma=False)
```

```python
import math

import jax
import jax.numpy as jnp
import numpy as np
from jax import lax
from jax.experimental import pallas as pl
from jax.experimental.pallas import tpu as pltpu
from jax.sharding import PartitionSpec as P

SMOOTH = 4


def from_behind(block, axis, distance):
    devices = range(lax.axis_size(axis))
    route = [(i - distance, i) for i in devices if i - distance in devices]
    return lax.ppermute(block, axis, route)


def column_bins(count, group_width):
    index = np.arange(count, dtype=np.int64)
    group = index // (2 * group_width)
    within = index % group_width
    is_imag = index // group_width % 2
    return (group * group_width + within, is_imag)


def forward_table(samples, bins, group_width):
    freq, is_imag = column_bins(2 * bins, group_width)
    moments = np.arange(samples, dtype=np.int64)[:, None]
    phase = (moments * freq[None, :] % samples).astype(np.float32) * np.float32(2.0 * math.pi / samples)
    phase = phase.astype(np.float64)
    table = np.where(is_imag[None, :] == 1, -np.sin(phase), np.cos(phase)).astype(np.float32)
    return jnp.asarray(table.astype(jnp.bfloat16))


def inverse_table(samples, bins, group_width, segments):
    freq, is_imag = column_bins(2 * bins, group_width)
    lag = np.arange(samples, dtype=np.int64) - samples // 2
    phase = np.mod(freq[:, None] * lag[None, :], samples).astype(np.float32) * np.float32(
        2.0 * math.pi / samples
    )
    phase = phase.astype(np.float64)
    weight = np.where(freq == 0, 1.0, 2.0).astype(np.float32) / np.float32(math.sqrt(samples * segments))
    wave = np.where(is_imag[:, None] == 1, -np.sin(phase), np.cos(phase)).astype(np.float32)
    return jnp.asarray((weight[:, None] * wave).astype(np.float32).astype(jnp.bfloat16))


def whiten_cols(spectra, groups):
    bins = spectra.shape[0] // 2
    width = bins // groups
    rest = spectra.shape[1:]
    split = spectra.reshape((groups, 2, width) + rest)
    real_part = split[:, 0].reshape((bins,) + rest)
    imag_part = split[:, 1].reshape((bins,) + rest)
    amplitude = jnp.sqrt(real_part * real_part + imag_part * imag_part)
    padded = jnp.pad(amplitude, [(SMOOTH, SMOOTH)] + [(0, 0)] * len(rest))
    triple = padded[: bins + 6] + padded[1 : bins + 7] + padded[2 : bins + 8]
    smooth = (triple[:bins] + triple[3 : bins + 3] + triple[6 : bins + 6]) / (2 * SMOOTH + 1)
    water = 0.8 * jnp.mean(amplitude, axis=0, keepdims=True) + 1e-06
    level = jnp.maximum(smooth, water).reshape((groups, 1, width) + rest)
    return (split / level).reshape(spectra.shape)


def cross_kernel(own_ref, next_ref, wrap_ref, out_ref):
    block = own_ref.shape[2]
    row = lax.broadcasted_iota(jnp.int32, (block, block), 0)
    col = lax.broadcasted_iota(jnp.int32, (block, block), 1)
    flip = (row + col == block - 1).astype(jnp.bfloat16)

    def reverse_rows(x):
        return jnp.dot(flip, x, preferred_element_type=jnp.float32).astype(jnp.bfloat16)

    for f in range(own_ref.shape[1]):
        own_real = own_ref[0, f].T
        own_imag = own_ref[1, f].T
        own_both = jnp.concatenate([own_real, own_imag], axis=1)
        lhs = jnp.concatenate(
            [own_both, jnp.concatenate([own_imag, -own_real], axis=1)], axis=0
        )
        next_both = jnp.concatenate(
            [(next_ref[0, f] + wrap_ref[0, f]).T, (next_ref[1, f] + wrap_ref[1, f]).T], axis=1
        )
        rhs = jnp.concatenate([reverse_rows(next_both), reverse_rows(own_both)], axis=0)
        both = lax.dot_general(
            lhs, rhs, (((1,), (1,)), ((), ())), preferred_element_type=jnp.float32
        )
        for part in range(2):
            rows = both[part * block : (part + 1) * block]
            sheared = pltpu.roll(rows, 1, 1, stride=1, stride_axis=0)[:, block:]
            ordered = jnp.dot(
                sheared.astype(jnp.bfloat16), flip, preferred_element_type=jnp.float32
            )
            out_ref[:, part, f] = ordered.reshape(out_ref.shape[0], -1, block).astype(out_ref.dtype)


def cross(own_t, next_t, wrap_t, parts, interpret=False):
    two, width, block, segs = own_t.shape
    step = min(width, 8)
    spec = pl.BlockSpec((two, step, block, segs), lambda i: (0, i, 0, 0))
    return pl.pallas_call(
        cross_kernel,
        grid=(width // step,),
        in_specs=[spec, spec, spec],
        out_specs=pl.BlockSpec(
            (parts, two, step, block // parts, block), lambda i: (0, 0, i, 0, 0)
        ),
        out_shape=jax.ShapeDtypeStruct((parts, two, width, block // parts, block), jnp.bfloat16),
        interpret=interpret,
    )(own_t, next_t, wrap_t)


CHUNKS = 2
ROW = 4


def body(traces, live):
    seg_dev, block, samples = traces.shape
    bins = samples // 2
    groups = lax.axis_size("tm")
    group_width = bins // groups
    width = group_width // CHUNKS
    segments = seg_dev * groups
    table = forward_table(samples, bins, group_width)
    inverse = inverse_table(samples, bins, group_width, segments).reshape(
        groups, 2, CHUNKS, width, samples
    )
    spectra = jnp.einsum("jat,tc->cja", traces, table, preferred_element_type=jnp.float32)
    flags = live.astype(jnp.float32)
    white = (whiten_cols(spectra, groups) * flags).astype(jnp.bfloat16)
    white = white.reshape(groups, 2, CHUNKS, width, seg_dev, block)
    blocks = lax.axis_size("chan")
    inner_route = [(i + 1, i) for i in range(blocks - 1) if (i + 1) % ROW != 0]
    wrap_route = [
        ((i + 1) * groups + m, i * groups + (m ^ 2))
        for i in range(blocks - 1)
        if (i + 1) % ROW == 0
        for m in range(groups)
    ]
    swapped = lax.axis_index("chan") < ROW

    def swap_pairs(x):
        split = x.reshape((groups // 4, 2, 2) + x.shape[1:])
        return jnp.where(swapped, split[:, ::-1], split).reshape(x.shape)

    lagged = None
    for chunk in range(CHUNKS):
        piece = swap_pairs(white[:, :, chunk]).reshape(groups * 2 * width, seg_dev, block)
        own = lax.all_to_all(piece, "tm", split_axis=0, concat_axis=1, tiled=True)
        own_t = own.reshape(2, width, segments, block)
        next_t = lax.ppermute(own_t, "chan", inner_route)
        wrap_t = lax.ppermute(own_t, ("chan", "tm"), wrap_route)
        stack = cross(own_t, next_t, wrap_t, groups)
        gathered = lax.all_to_all(stack, "tm", split_axis=0, concat_axis=0, tiled=True)
        gathered = gathered.reshape(groups * 2 * width, block // groups, block)
        rows = swap_pairs(inverse[:, :, chunk]).reshape(groups * 2 * width, samples)
        part = jnp.einsum("hak,hl->akl", gathered, rows, preferred_element_type=jnp.float32)
        lagged = part if lagged is None else lagged + part
    return lagged.astype(jnp.bfloat16)


def solution(mesh):
    in_specs = (P("tm", "chan", None), P("chan"))
    out_specs = P(("chan", "tm"), None, None)
    return jax.shard_map(body, mesh=mesh, in_specs=in_specs, out_specs=out_specs, check_vma=False)
```

```python
import math

import jax
import jax.numpy as jnp
import numpy as np
from jax import lax
from jax.experimental import pallas as pl
from jax.experimental.pallas import tpu as pltpu
from jax.sharding import PartitionSpec as P

SMOOTH = 4


def from_behind(block, axis, distance):
    devices = range(lax.axis_size(axis))
    route = [(i - distance, i) for i in devices if i - distance in devices]
    return lax.ppermute(block, axis, route)


def column_bins(count, group_width):
    index = np.arange(count, dtype=np.int64)
    group = index // (2 * group_width)
    within = index % group_width
    is_imag = index // group_width % 2
    return (group * group_width + within, is_imag)


def forward_table(samples, bins, group_width):
    freq, is_imag = column_bins(2 * bins, group_width)
    moments = np.arange(samples, dtype=np.int64)[:, None]
    phase = (moments * freq[None, :] % samples).astype(np.float32) * np.float32(2.0 * math.pi / samples)
    phase = phase.astype(np.float64)
    table = np.where(is_imag[None, :] == 1, -np.sin(phase), np.cos(phase)).astype(np.float32)
    return jnp.asarray(table.astype(jnp.bfloat16))


def inverse_table(samples, bins, group_width, segments):
    freq, is_imag = column_bins(2 * bins, group_width)
    lag = np.arange(samples, dtype=np.int64) - samples // 2
    phase = np.mod(freq[:, None] * lag[None, :], samples).astype(np.float32) * np.float32(
        2.0 * math.pi / samples
    )
    phase = phase.astype(np.float64)
    weight = np.where(freq == 0, 1.0, 2.0).astype(np.float32) / np.float32(math.sqrt(samples * segments))
    wave = np.where(is_imag[:, None] == 1, -np.sin(phase), np.cos(phase)).astype(np.float32)
    return jnp.asarray((weight[:, None] * wave).astype(np.float32).astype(jnp.bfloat16))


def whiten_cols(spectra, groups):
    bins = spectra.shape[0] // 2
    width = bins // groups
    rest = spectra.shape[1:]
    split = spectra.reshape((groups, 2, width) + rest)
    real_part = split[:, 0].reshape((bins,) + rest)
    imag_part = split[:, 1].reshape((bins,) + rest)
    amplitude = jnp.sqrt(real_part * real_part + imag_part * imag_part)
    padded = jnp.pad(amplitude, [(SMOOTH, SMOOTH)] + [(0, 0)] * len(rest))
    triple = padded[: bins + 6] + padded[1 : bins + 7] + padded[2 : bins + 8]
    smooth = (triple[:bins] + triple[3 : bins + 3] + triple[6 : bins + 6]) / (2 * SMOOTH + 1)
    water = 0.8 * jnp.mean(amplitude, axis=0, keepdims=True) + 1e-06
    level = jnp.maximum(smooth, water).reshape((groups, 1, width) + rest)
    return (split / level).reshape(spectra.shape)


def cross_kernel(own_ref, next_ref, wrap_ref, out_ref):
    block = own_ref.shape[2]
    row = lax.broadcasted_iota(jnp.int32, (block, block), 0)
    col = lax.broadcasted_iota(jnp.int32, (block, block), 1)
    flip = (row + col == block - 1).astype(jnp.bfloat16)

    def reverse_rows(x):
        return jnp.dot(flip, x, preferred_element_type=jnp.float32).astype(jnp.bfloat16)

    for f in range(own_ref.shape[1]):
        own_real = own_ref[0, f].T
        own_imag = own_ref[1, f].T
        own_both = jnp.concatenate([own_real, own_imag], axis=1)
        lhs = jnp.concatenate(
            [own_both, jnp.concatenate([own_imag, -own_real], axis=1)], axis=0
        )
        next_both = jnp.concatenate(
            [(next_ref[0, f] + wrap_ref[0, f]).T, (next_ref[1, f] + wrap_ref[1, f]).T], axis=1
        )
        rhs = jnp.concatenate([reverse_rows(next_both), reverse_rows(own_both)], axis=0)
        both = lax.dot_general(
            lhs, rhs, (((1,), (1,)), ((), ())), preferred_element_type=jnp.float32
        )
        for part in range(2):
            rows = both[part * block : (part + 1) * block]
            sheared = pltpu.roll(rows, 1, 1, stride=1, stride_axis=0)[:, block:]
            ordered = jnp.dot(
                sheared.astype(jnp.bfloat16), flip, preferred_element_type=jnp.float32
            )
            out_ref[:, part, f] = ordered.reshape(out_ref.shape[0], -1, block).astype(out_ref.dtype)


def cross(own_t, next_t, wrap_t, parts, interpret=False):
    two, width, block, segs = own_t.shape
    step = min(width, 16)
    spec = pl.BlockSpec((two, step, block, segs), lambda i: (0, i, 0, 0))
    return pl.pallas_call(
        cross_kernel,
        grid=(width // step,),
        in_specs=[spec, spec, spec],
        out_specs=pl.BlockSpec(
            (parts, two, step, block // parts, block), lambda i: (0, 0, i, 0, 0)
        ),
        out_shape=jax.ShapeDtypeStruct((parts, two, width, block // parts, block), jnp.bfloat16),
        interpret=interpret,
    )(own_t, next_t, wrap_t)


CHUNKS = 2
ROW = 4


def body(traces, live):
    seg_dev, block, samples = traces.shape
    bins = samples // 2
    groups = lax.axis_size("tm")
    group_width = bins // groups
    width = group_width // CHUNKS
    segments = seg_dev * groups
    table = forward_table(samples, bins, group_width)
    inverse = inverse_table(samples, bins, group_width, segments).reshape(
        groups, 2, CHUNKS, width, samples
    )
    spectra = jnp.einsum("jat,tc->cja", traces, table, preferred_element_type=jnp.float32)
    flags = live.astype(jnp.float32)
    white = (whiten_cols(spectra, groups) * flags).astype(jnp.bfloat16)
    white = white.reshape(groups, 2, CHUNKS, width, seg_dev, block)
    blocks = lax.axis_size("chan")
    inner_route = [(i + 1, i) for i in range(blocks - 1) if (i + 1) % ROW != 0]
    wrap_route = [
        ((i + 1) * groups + m, i * groups + (m ^ 2))
        for i in range(blocks - 1)
        if (i + 1) % ROW == 0
        for m in range(groups)
    ]
    swapped = lax.axis_index("chan") < ROW

    def swap_pairs(x):
        split = x.reshape((groups // 4, 2, 2) + x.shape[1:])
        return jnp.where(swapped, split[:, ::-1], split).reshape(x.shape)

    lagged = None
    for chunk in range(CHUNKS):
        piece = swap_pairs(white[:, :, chunk]).reshape(groups * 2 * width, seg_dev, block)
        own = lax.all_to_all(piece, "tm", split_axis=0, concat_axis=1, tiled=True)
        own_t = own.reshape(2, width, segments, block)
        next_t = lax.ppermute(own_t, "chan", inner_route)
        wrap_t = lax.ppermute(own_t, ("chan", "tm"), wrap_route)
        stack = cross(own_t, next_t, wrap_t, groups)
        gathered = lax.all_to_all(stack, "tm", split_axis=0, concat_axis=0, tiled=True)
        gathered = gathered.reshape(groups * 2 * width, block // groups, block)
        rows = swap_pairs(inverse[:, :, chunk]).reshape(groups * 2 * width, samples)
        part = jnp.einsum("hak,hl->akl", gathered, rows, preferred_element_type=jnp.float32)
        lagged = part if lagged is None else lagged + part
    return lagged.astype(jnp.bfloat16)


def solution(mesh):
    in_specs = (P("tm", "chan", None), P("chan"))
    out_specs = P(("chan", "tm"), None, None)
    return jax.shard_map(body, mesh=mesh, in_specs=in_specs, out_specs=out_specs, check_vma=False)
```
